32 devices in a mesh: dp: 1, tensor: 32 (over z, y, x, core).
Axes of the slice: x: 2, y: 2, z: 4, core: 2. Of those that a mesh axis runs over, the one named last changes fastest.
Arguments:
- hidden: bfloat16 [1024, 2048], P(('dp', 'tensor')), may hold values from -6 to 6
- norm_gain: bfloat16 [2048], replicated, may hold values from 0.099609375 to 1.8984375
- router_weight: bfloat16 [2048, 8], replicated, may hold values from -0.125 to 0.125
- kv_weight: bfloat16 [2048, 4096], P(None, 'tensor'), may hold values from -0.125 to 0.125
- query_weight: bfloat16 [2048, 16384], P(None, 'tensor'), may hold values from -0.125 to 0.125
- out_weight: bfloat16 [16384, 2048], P('tensor'), may hold values from -0.5 to 0.5
- routes: int32 [1024, 2], P('dp'), may hold values from 0 to 7, all different within a row; in each aligned block of 1024 rows (0 to 1023, 1024 to 2047, ...) at most 384 rows name the same one
- segment_ids: int32 [1024], P('dp'), may hold values from 0 to 3, never falling along the last dimension, each value on 1 to 512 neighbouring positions
- page_table: int32 [8], P('dp'), may hold values from 0 to 15, as said below
- kv_cache: bfloat16 [16, 128, 4096], P('dp', None, 'tensor'), may hold values from -6 to 6
Outputs:
- attended_out: bfloat16 [1024, 2048], P(('dp', 'tensor'))
- new_cache: bfloat16 [16, 128, 4096], P('dp', None, 'tensor')
The draws below stay inside these ranges and needn't reach their ends.
Inputs may be any that keep to these rules, and one draw needn't show every extreme that they name: `routes`: no expert is named by more than 384 tokens of a batch, and one is named by exactly 384; a token names two different experts. `segment_ids`: ids never fall along the pack; each prompt has 1 to 512 tokens and one has exactly 512. `page_table`: distinct pages.
All inputs are finite; a program needn't handle non-finite values.
Results may differ from the reference program's by a relative error of at most 0.025.
Values may be sent and summed in bfloat16 or wider, within the bound.
No kernel may reach another device: no remote copies, remote signals or barrier semaphores. Data moves between devices by JAX's collectives and lax.ppermute only.
A program may use at most 128 MiB of HBM per device.

```python
import math
import jax
import jax.numpy as jnp
import numpy as np
from jax import lax

D = 2048
HD = 128
KVH = 16
EA = 8
TOPK = 2
PAGE = 128
S = 1024
CAP = 384
BLOCKS = 8
NPAGES = 16
SEGS = 4
SEG_MOST = 512
N_TENSOR = 32


def draw_page_table(key, part):
    return jax.random.permutation(key, NPAGES)[:BLOCKS].astype(jnp.int32)


def block_scale(key, extent, pieces, smallest, top_value):
    level = 1.0
    for axis_at, blocks in pieces:
        draws = jax.random.uniform(jax.random.fold_in(jax.random.fold_in(key, 6), axis_at), (blocks,), jnp.float32, smallest / len(pieces), top_value / len(pieces))
        level = level * jnp.repeat(jnp.exp(draws), extent[axis_at] // blocks).reshape((-1,) + (1,) * (len(extent) - 1 - axis_at))
    return level


def split_up(amount, total, limit, lean):
    loads = [(1 << 20) // math.isqrt(rank ** lean) + 1 for rank in range(2, amount + 1)]
    spare, counts = total - limit - (amount - 1), [1] * (amount - 1)
    while spare > 0:
        free = [i for i in range(amount - 1) if counts[i] < limit]
        whole, left = sum([loads[i] for i in free]), spare
        for i in free:
            addition = min(limit - counts[i], max(1, left * loads[i] // whole), spare)
            counts[i] = counts[i] + addition
            spare = spare - addition
    return np.array([limit] + counts)


def uneven_parts(stream_key, amount, total, limit, slope):
    if amount == 2:
        one = jax.random.randint(stream_key, (), max(1, total - limit), min(limit, total - 1) + 1)
        return jnp.stack([one, total - one])
    lengths = jnp.asarray(split_up(amount, total, limit, slope), jnp.int32)
    couples = (amount - 1) // 2
    giver, receiver = lengths[1:1 + 2 * couples:2], lengths[2:2 + 2 * couples:2]
    room = jnp.minimum(giver - 1, limit - receiver)
    moved = jax.random.randint(jax.random.fold_in(stream_key, 1), (couples,), 0, 1 << 20) % (room + 1)
    lengths = lengths.at[1:1 + 2 * couples:2].set(giver - moved).at[2:2 + 2 * couples:2].set(receiver + moved)
    return lengths[jax.random.permutation(jax.random.fold_in(stream_key, 2), amount)]


def assign_block(own_key, own, number, rows, amount, top, reach, slope):
    sequence = jax.random.permutation(own_key, amount)
    heavy_load, usual = shares(amount, rows * top, reach, slope, True), shares(amount, rows * top, reach, slope, False)
    places = jnp.arange(amount)

    def named(sizes, rotation):
        used = int((sizes > 0).sum())
        fixed = max(1, used // 4)
        shifted = fixed + (places - fixed + rotation * (used - fixed)) % max(1, amount - fixed)
        return jnp.zeros((amount,), jnp.int32).at[sequence[jnp.where(places < fixed, places, shifted)]].set(jnp.asarray(sizes, jnp.int32))

    sizes = jnp.where(number % 4 == 0, named(heavy_load, number // 4), named(usual, number - number // 4 - 1))
    mixed = jax.random.permutation(jax.random.fold_in(own, 3), amount)
    donor, sink = mixed[0:amount // 2 * 2:2], mixed[1:amount // 2 * 2:2]
    room = jnp.minimum(sizes[donor] - 1, reach - sizes[sink]) // 2
    room = jnp.where((donor == sequence[0]) | (sink == sequence[0]) | (sizes[sink] == 0), 0, jnp.maximum(room, 0))
    shifted = jax.random.randint(jax.random.fold_in(own, 4), (amount // 2,), 0, 1 << 20) % (room + 1)
    sizes = sizes.at[donor].add(-shifted).at[sink].add(shifted)
    items = jnp.searchsorted(jnp.cumsum(sizes), jnp.arange(rows * top), side="right").astype(jnp.int32)
    listing = items.reshape(top, rows).T
    listing = listing[jax.random.permutation(jax.random.fold_in(own, 1), rows)]
    rotation = jax.random.randint(jax.random.fold_in(own, 2), (rows, 1), 0, top)
    return jnp.take_along_axis(listing, (jnp.arange(top)[None, :] + rotation) % top, axis=1)


def shares(number_of, total, most, skew, full):
    weights = [(1 << 20) // math.isqrt(rank ** skew) + 1 for rank in range(1, number_of + 1)]
    largest = most if full else min(most, max(-(-total // number_of), total * weights[0] // sum(weights)))
    least = 1 if total - largest >= number_of - 1 else 0
    counts, rest = [largest] + [least] * (number_of - 1), total - largest - least * (number_of - 1)
    while rest > 0:
        movable = [i for i in range(1, number_of) if counts[i] < largest] or [i for i in range(1, number_of) if counts[i] < most]
        whole, budget = sum([weights[i] for i in movable]), rest
        for i in movable:
            extra = min(most - counts[i], max(1, budget * weights[i] // whole), rest)
            counts[i] = counts[i] + extra
            rest = rest - extra
    return np.array(counts)


def noise(stream_key, shape, deviation, limit, cuts=(), kind=jnp.bfloat16):
    drawn = deviation * jax.random.normal(stream_key, shape, jnp.float32)
    if cuts:
        drawn = drawn * block_scale(stream_key, shape, cuts, -0.22, 0.18)
    return jnp.clip(drawn, -limit, limit).astype(kind)


def setup_inputs(seed: int = 0, part: int = 0) -> dict:
    keys = jax.random.split(jax.random.key(seed), 11)
    part_keys = jax.random.split(jax.random.fold_in(keys[10], part), 11)
    hidden = noise(part_keys[0], (S, D), 1.0, 6.0, ((0, 32),))
    norm_gain = jnp.clip(1.0 + 0.18 * jax.random.normal(keys[1], (D,), jnp.float32), 0.099609375, 1.8984375).astype(jnp.bfloat16)
    router_weight = noise(keys[2], (D, EA), D ** -0.5, 0.125)
    kv_weight = noise(keys[3], (D, 2 * KVH * HD), D ** -0.5, 0.125, ((1, 32),))
    query_weight = noise(keys[4], (D, KVH * EA * HD), D ** -0.5, 0.125, ((1, 32),))
    out_weight = noise(keys[5], (KVH * EA * HD, D), HD ** -0.5, 0.5, ((0, 32),))
    routes_keys = jax.random.split(jax.random.fold_in(part_keys[6], 1), S // S)
    routes_turns = jax.random.permutation(jax.random.fold_in(part_keys[6], 3), S // S)
    routes = jax.vmap(lambda own, number: assign_block(jax.random.fold_in(part_keys[6], 2), own, number, S, EA, TOPK, CAP, 2))(routes_keys, routes_turns).reshape((S, TOPK))
    segment_ids = jnp.searchsorted(jnp.cumsum(uneven_parts(part_keys[7], SEGS, S, SEG_MOST, 2)), jnp.arange(S), side="right").astype(jnp.int32)
    page_table = draw_page_table(jax.random.fold_in(jax.random.fold_in(keys[10], part), 71), part)
    kv_cache = noise(part_keys[9], (NPAGES, PAGE, 2 * KVH * HD), 1.0, 6.0, ((2, 32),))
    return {"hidden": hidden, "norm_gain": norm_gain, "router_weight": router_weight, "kv_weight": kv_weight, "query_weight": query_weight, "out_weight": out_weight, "routes": routes, "segment_ids": segment_ids, "page_table": page_table, "kv_cache": kv_cache}


def normalize(hidden, norm_gain):
    values = hidden.astype(jnp.float32)
    factor = lax.rsqrt(lax.optimization_barrier(jnp.mean(values * values, axis=-1, keepdims=True)) + 1e-05)
    return (values * factor * norm_gain.astype(jnp.float32)).astype(jnp.bfloat16)

def gate_table(normed, router_weight, routes):
    logits = jnp.dot(normed, router_weight, preferred_element_type=jnp.float32)
    chosen = jnp.take_along_axis(logits, routes, axis=1)
    weights = jax.nn.softmax(chosen, axis=-1)
    expert_ids = jnp.arange(router_weight.shape[1], dtype=jnp.int32)
    onehot = (routes[:, :, None] == expert_ids[None, None, :]).astype(jnp.float32)
    return lax.optimization_barrier(jnp.sum(weights[:, :, None] * onehot, axis=1))

def positions_of(segment_ids):
    index_row = jnp.arange(segment_ids.shape[0], dtype=jnp.int32)
    starts_here = jnp.concatenate([jnp.ones((1,), dtype=bool), segment_ids[1:] != segment_ids[:-1]])
    segment_start = lax.cummax(jnp.where(starts_here, index_row, 0), axis=0)
    return index_row - segment_start

def rotate(values, positions):
    half_width = values.shape[-1] // 2
    frequency = 10000.0 ** (-jnp.arange(half_width, dtype=jnp.float32) / half_width)
    angles = positions.astype(jnp.float32)[:, None] * frequency[None, :]
    angles = angles.reshape((values.shape[0],) + (1,) * (values.ndim - 2) + (half_width,))
    cosine = jnp.cos(angles)
    sine_part = jnp.sin(angles)
    leading = values[..., :half_width]
    trailing = values[..., half_width:]
    return jnp.concatenate([leading * cosine - trailing * sine_part, trailing * cosine + leading * sine_part], axis=-1)

def expert_slots(routes, expert, capacity):
    is_hit = jnp.any(routes == expert, axis=1)
    running = jnp.cumsum(is_hit.astype(jnp.int32))
    placed = jnp.where(is_hit, running - 1, capacity)
    index_row = jnp.arange(routes.shape[0], dtype=jnp.int32)
    slot_tok = jnp.zeros((capacity + 1,), jnp.int32).at[placed].set(index_row)[:capacity]
    is_valid = jnp.arange(capacity, dtype=jnp.int32) < running[-1]
    return (slot_tok, is_valid)

def attend(queries, key_rows, value_rows, allowed):
    scores = jnp.dot(queries, key_rows.T, preferred_element_type=jnp.float32)
    scores = jnp.where(allowed, scores, -1e+30)
    probabilities = jax.nn.softmax(scores, axis=-1).astype(jnp.bfloat16)
    return jnp.dot(probabilities, value_rows, preferred_element_type=jnp.float32)

def reference(hidden, norm_gain, router_weight, kv_weight, query_weight, out_weight, routes, segment_ids, page_table, kv_cache):
    normed = normalize(hidden, norm_gain)
    gates = gate_table(normed, router_weight, routes)
    positions = positions_of(segment_ids)
    kv_full = jnp.dot(normed, kv_weight, preferred_element_type=jnp.float32).reshape(S, KVH, 2, HD)
    kv_rows = jnp.stack([rotate(kv_full[:, :, 0], positions), kv_full[:, :, 1]], axis=2).astype(jnp.bfloat16)
    new_cache = kv_cache.at[page_table].set(kv_rows.reshape(BLOCKS, PAGE, KVH * 2 * HD))
    key_all = kv_rows[:, :, 0]
    value_all = kv_rows[:, :, 1]
    index_row = jnp.arange(S, dtype=jnp.int32)
    per_group = KVH * EA // N_TENSOR
    scale_factor = HD ** (-0.5)

    def pair_term(partial_value, pair):
        head_index = pair // EA
        expert = pair % EA
        slot_tok, is_valid = expert_slots(routes, expert, CAP)
        queries = jnp.dot(normed[slot_tok], lax.dynamic_slice_in_dim(query_weight, pair * HD, HD, 1), preferred_element_type=jnp.float32)
        queries = (rotate(queries, positions[slot_tok]) * scale_factor).astype(jnp.bfloat16)
        keys_here = lax.dynamic_index_in_dim(key_all, head_index, 1, keepdims=False)
        values_here = lax.dynamic_index_in_dim(value_all, head_index, 1, keepdims=False)
        allowed = (segment_ids[slot_tok][:, None] == segment_ids[None, :]) & (index_row[None, :] <= slot_tok[:, None])
        attended = attend(queries, keys_here, values_here, allowed)
        gate_here = gates[slot_tok, expert] * is_valid.astype(jnp.float32)
        gated = (attended * gate_here[:, None]).astype(jnp.bfloat16)
        term_rows = jnp.dot(gated, lax.dynamic_slice_in_dim(out_weight, pair * HD, HD, 0), preferred_element_type=jnp.float32)
        target = jnp.where(is_valid, slot_tok, S)
        return (partial_value.at[target].add(term_rows, mode='drop'), None)

    def group_term(total, group):
        pairs_here = group * per_group + jnp.arange(per_group, dtype=jnp.int32)
        partial_value, _ = lax.scan(pair_term, jnp.zeros((S, D), jnp.float32), pairs_here)
        rounded = lax.optimization_barrier(partial_value.astype(jnp.bfloat16))
        return (total + rounded.astype(jnp.float32), None)
    total, _ = lax.scan(group_term, jnp.zeros((S, D), jnp.float32), jnp.arange(N_TENSOR, dtype=jnp.int32))
    attended_out = (hidden.astype(jnp.float32) + total).astype(jnp.bfloat16)
    return (attended_out, new_cache)
```

```python
import jax
import jax.numpy as jnp
from jax import lax
from jax.sharding import PartitionSpec as P

D = 2048
HD = 128
EA = 8
PAGE = 128
REDUCE_PARTS = 4


def swapped(array, axis, bit):
    return lax.ppermute(array, axis, [(i, i ^ 1 << bit) for i in range(lax.axis_size(axis))])


def normalize(hidden, norm_gain):
    values = hidden.astype(jnp.float32)
    factor = lax.rsqrt(jnp.mean(values * values, axis=-1, keepdims=True) + 1e-05)
    return (values * factor * norm_gain.astype(jnp.float32)).astype(jnp.bfloat16)


def gate_table(normed, router_weight, routes):
    logits = jnp.dot(normed, router_weight, preferred_element_type=jnp.float32)
    expert_ids = jnp.arange(router_weight.shape[1], dtype=jnp.int32)
    onehot = routes[:, :, None] == expert_ids[None, None, :]
    chosen = jnp.sum(jnp.where(onehot, logits[:, None, :], 0.0), axis=2)
    weights = jax.nn.softmax(chosen, axis=-1)
    return jnp.sum(jnp.where(onehot, weights[:, :, None], 0.0), axis=1)


def positions_of(segment_ids):
    index_row = jnp.arange(segment_ids.shape[0], dtype=jnp.int32)
    starts_here = jnp.concatenate([jnp.ones((1,), dtype=bool), segment_ids[1:] != segment_ids[:-1]])
    segment_start = lax.cummax(jnp.where(starts_here, index_row, 0), axis=0)
    return index_row - segment_start


def rotate(values, positions):
    half_width = values.shape[-1] // 2
    frequency = 10000.0 ** (-jnp.arange(half_width, dtype=jnp.float32) / half_width)
    angles = positions.astype(jnp.float32)[:, None] * frequency[None, :]
    angles = angles.reshape((values.shape[0],) + (1,) * (values.ndim - 2) + (half_width,))
    cosine = jnp.cos(angles)
    sine_part = jnp.sin(angles)
    leading = values[..., :half_width]
    trailing = values[..., half_width:]
    return jnp.concatenate(
        [leading * cosine - trailing * sine_part, trailing * cosine + leading * sine_part], axis=-1
    )


def project_kv(normed, weight, positions, first_block):
    projected = jnp.dot(normed, weight, preferred_element_type=jnp.float32)
    block_total = weight.shape[1] // HD
    blocks = projected.reshape(normed.shape[0], block_total, HD)
    block_index = first_block + jnp.arange(block_total, dtype=jnp.int32)
    turned = rotate(blocks, positions)
    chosen = jnp.where((block_index % 2 == 0)[None, :, None], turned, blocks)
    return chosen.astype(jnp.bfloat16).reshape(normed.shape[0], weight.shape[1])


def write_pages(kv_cache, page_table, rows):
    pages = jnp.arange(kv_cache.shape[0], dtype=jnp.int32)
    hit = page_table[None, :] == pages[:, None]
    placed = jnp.einsum(
        "pb,brc->prc", hit.astype(rows.dtype), rows, preferred_element_type=jnp.float32
    ).astype(kv_cache.dtype)
    return jnp.where(jnp.any(hit, axis=1)[:, None, None], placed, kv_cache)


def bit_orders(bits, parts):
    rest = list(range(1, bits))
    if not rest:
        return [[0]] * parts
    return [[0] + rest[j % len(rest):] + rest[:j % len(rest)] for j in range(parts)]


def reduce_to_owner(partial, axis):
    size = lax.axis_size(axis)
    bits = size.bit_length() - 1
    assert 1 << bits == size
    me = lax.axis_index(axis)
    rows, width = partial.shape
    block = rows // size
    parts = REDUCE_PARTS if width % REDUCE_PARTS == 0 else 1
    piece = width // parts
    outs = []
    for j, order in enumerate(bit_orders(bits, parts)):
        cols = partial[:, j * piece:(j + 1) * piece]
        cube = cols.reshape((2,) * bits + (block, piece))
        cube = jnp.transpose(cube, [bits - 1 - k for k in order] + [bits, bits + 1])
        current = cube.reshape(rows, piece)
        for k in order:
            half = current.shape[0] // 2
            mine = (me >> k) & 1
            keep = lax.dynamic_slice_in_dim(current, mine * half, half, 0)
            send = lax.dynamic_slice_in_dim(current, (1 - mine) * half, half, 0)
            got = lax.ppermute(send, axis, [(i, i ^ (1 << k)) for i in range(size)])
            current = (keep.astype(jnp.float32) + got.astype(jnp.float32)).astype(jnp.bfloat16)
        outs.append(current)
    return jnp.concatenate(outs, axis=1)


def local(
    hidden,
    norm_gain,
    router_weight,
    kv_weight,
    query_weight,
    out_weight,
    routes,
    segment_ids,
    page_table,
    kv_cache,
):
    device_index = lax.axis_index("tensor")
    token_count = routes.shape[0]
    normed = lax.all_gather(normalize(hidden, norm_gain), "tensor", axis=0, tiled=True)
    gates = gate_table(normed, router_weight, routes)
    positions = positions_of(segment_ids)
    kv_width = kv_weight.shape[1]
    block_count = kv_width // HD
    own_rows = project_kv(normed, kv_weight, positions, device_index * block_count)
    new_cache = write_pages(kv_cache, page_table, own_rows.reshape(page_table.shape[0], PAGE, kv_width))
    partner_rows = swapped(own_rows, "tensor", 0)
    leading_first = device_index % 2 == 0
    head_rows = jnp.where(
        leading_first,
        jnp.concatenate([own_rows, partner_rows], axis=1),
        jnp.concatenate([partner_rows, own_rows], axis=1),
    )
    local_heads = head_rows.shape[1] // (2 * HD)
    head_rows = head_rows.reshape(token_count, local_heads, 2, HD)
    pair_count = query_weight.shape[1] // HD
    local_experts = pair_count // local_heads
    index_row = jnp.arange(token_count, dtype=jnp.int32)
    scale_factor = HD ** (-0.5)
    queries = jnp.dot(normed, query_weight, preferred_element_type=jnp.float32)
    queries = queries.reshape(token_count, local_experts, HD)
    queries = (rotate(queries, positions) * scale_factor).astype(jnp.bfloat16)
    allowed = (segment_ids[:, None] == segment_ids[None, :]) & (index_row[None, :] <= index_row[:, None])
    scores = jnp.einsum(
        "teh,sh->ets", queries, head_rows[:, 0, 0], preferred_element_type=jnp.float32
    )
    scores = jnp.where(allowed[None], scores, -1e30)
    probabilities = jax.nn.softmax(scores, axis=-1).astype(jnp.bfloat16)
    attended = jnp.einsum(
        "ets,sh->teh", probabilities, head_rows[:, 0, 1], preferred_element_type=jnp.float32
    )
    first_expert = (device_index * pair_count) % EA
    gate_here = lax.dynamic_slice_in_dim(gates, first_expert, local_experts, 1)
    gated = (attended * gate_here[:, :, None]).astype(jnp.bfloat16)
    flat = gated.reshape(token_count, pair_count * HD)
    partial = jnp.dot(flat, out_weight, preferred_element_type=jnp.float32).astype(jnp.bfloat16)
    reduced = reduce_to_owner(partial, "tensor").astype(jnp.float32)
    attended_out = (hidden.astype(jnp.float32) + reduced).astype(jnp.bfloat16)
    return (attended_out, new_cache)


def solution(mesh):
    placed = (
        P(("dp", "tensor"), None),
        P(),
        P(),
        P(None, "tensor"),
        P(None, "tensor"),
        P("tensor", None),
        P("dp", None),
        P("dp"),
        P("dp"),
        P("dp", None, "tensor"),
    )
    return jax.shard_map(
        local,
        mesh=mesh,
        in_specs=placed,
        out_specs=(P(("dp", "tensor"), None), P("dp", None, "tensor")),
        check_vma=False,
    )
```

```python
import jax
import jax.numpy as jnp
from jax import lax
from jax.experimental import pallas as pl
from jax.experimental.pallas import tpu as pltpu
from jax.sharding import PartitionSpec as P

D = 2048
HD = 128
EA = 8
PAGE = 128
REDUCE_PARTS = 4
SEG_MOST = 512
CHUNK = 128


def swapped(array, axis, bit):
    return lax.ppermute(array, axis, [(i, i ^ 1 << bit) for i in range(lax.axis_size(axis))])


def normalize(hidden, norm_gain):
    values = hidden.astype(jnp.float32)
    factor = lax.rsqrt(jnp.mean(values * values, axis=-1, keepdims=True) + 1e-05)
    return (values * factor * norm_gain.astype(jnp.float32)).astype(jnp.bfloat16)


def gate_table(normed, router_weight, routes):
    logits = jnp.dot(normed, router_weight, preferred_element_type=jnp.float32)
    expert_ids = jnp.arange(router_weight.shape[1], dtype=jnp.int32)
    onehot = routes[:, :, None] == expert_ids[None, None, :]
    chosen = jnp.sum(jnp.where(onehot, logits[:, None, :], 0.0), axis=2)
    weights = jax.nn.softmax(chosen, axis=-1)
    return jnp.sum(jnp.where(onehot, weights[:, :, None], 0.0), axis=1)


def positions_of(segment_ids):
    index_row = jnp.arange(segment_ids.shape[0], dtype=jnp.int32)
    starts_here = jnp.concatenate([jnp.ones((1,), dtype=bool), segment_ids[1:] != segment_ids[:-1]])
    segment_start = lax.cummax(jnp.where(starts_here, index_row, 0), axis=0)
    return index_row - segment_start


def rotate(values, positions):
    half_width = values.shape[-1] // 2
    frequency = 10000.0 ** (-jnp.arange(half_width, dtype=jnp.float32) / half_width)
    angles = positions.astype(jnp.float32)[:, None] * frequency[None, :]
    angles = angles.reshape((values.shape[0],) + (1,) * (values.ndim - 2) + (half_width,))
    cosine = jnp.cos(angles)
    sine_part = jnp.sin(angles)
    leading = values[..., :half_width]
    trailing = values[..., half_width:]
    return jnp.concatenate(
        [leading * cosine - trailing * sine_part, trailing * cosine + leading * sine_part], axis=-1
    )


def project_kv(normed, weight, positions, first_block):
    projected = jnp.dot(normed, weight, preferred_element_type=jnp.float32)
    block_total = weight.shape[1] // HD
    blocks = projected.reshape(normed.shape[0], block_total, HD)
    block_index = first_block + jnp.arange(block_total, dtype=jnp.int32)
    turned = rotate(blocks, positions)
    chosen = jnp.where((block_index % 2 == 0)[None, :, None], turned, blocks)
    return chosen.astype(jnp.bfloat16).reshape(normed.shape[0], weight.shape[1])


def write_pages(kv_cache, page_table, rows):
    pages = jnp.arange(kv_cache.shape[0], dtype=jnp.int32)
    hit = page_table[None, :] == pages[:, None]
    placed = jnp.einsum(
        "pb,brc->prc", hit.astype(rows.dtype), rows, preferred_element_type=jnp.float32
    ).astype(kv_cache.dtype)
    return jnp.where(jnp.any(hit, axis=1)[:, None, None], placed, kv_cache)


def bit_orders(bits, parts):
    rest = list(range(1, bits))
    if not rest:
        return [[0]] * parts
    return [[0] + rest[j % len(rest):] + rest[:j % len(rest)] for j in range(parts)]


def reduce_to_owner(partial, axis):
    size = lax.axis_size(axis)
    bits = size.bit_length() - 1
    assert 1 << bits == size
    me = lax.axis_index(axis)
    rows, width = partial.shape
    block = rows // size
    parts = REDUCE_PARTS if width % REDUCE_PARTS == 0 else 1
    piece = width // parts
    outs = []
    for j, order in enumerate(bit_orders(bits, parts)):
        cols = partial[:, j * piece:(j + 1) * piece]
        cube = cols.reshape((2,) * bits + (block, piece))
        cube = jnp.transpose(cube, [bits - 1 - k for k in order] + [bits, bits + 1])
        current = cube.reshape(rows, piece)
        for k in order:
            half = current.shape[0] // 2
            mine = (me >> k) & 1
            keep = lax.dynamic_slice_in_dim(current, mine * half, half, 0)
            send = lax.dynamic_slice_in_dim(current, (1 - mine) * half, half, 0)
            got = lax.ppermute(send, axis, [(i, i ^ (1 << k)) for i in range(size)])
            current = (keep.astype(jnp.float32) + got.astype(jnp.float32)).astype(jnp.bfloat16)
        outs.append(current)
    return jnp.concatenate(outs, axis=1)


def attention_kernel(window, q_ref, k_ref, v_ref, qseg_ref, kseg_ref, gate_ref, out_ref):
    chunk = pl.program_id(0)
    blocks = pl.num_programs(0)
    start_block = jnp.clip(chunk - (window - 1), 0, blocks - window)
    start = pl.multiple_of(start_block * CHUNK, CHUNK)
    span = window * CHUNK
    keys = k_ref[pl.ds(start, span), :]
    values = v_ref[pl.ds(start, span), :]
    key_seg = kseg_ref[:, pl.ds(start, span)]
    query_seg = qseg_ref[...]
    query_index = chunk * CHUNK + lax.broadcasted_iota(jnp.int32, (CHUNK, span), 0)
    key_index = start + lax.broadcasted_iota(jnp.int32, (CHUNK, span), 1)
    allowed = (query_seg == key_seg) & (key_index <= query_index)
    experts = gate_ref.shape[0]
    for e in range(experts):
        queries = q_ref[:, e * HD:(e + 1) * HD]
        scores = lax.dot_general(
            queries, keys, (((1,), (1,)), ((), ())), preferred_element_type=jnp.float32
        )
        scores = jnp.where(allowed, scores, -1e30)
        top = jnp.max(scores, axis=1, keepdims=True)
        raised = jnp.exp(scores - top)
        probabilities = (raised / jnp.sum(raised, axis=1, keepdims=True)).astype(jnp.bfloat16)
        attended = jnp.dot(probabilities, values, preferred_element_type=jnp.float32)
        out_ref[:, e * HD:(e + 1) * HD] = (attended * gate_ref[e]).astype(out_ref.dtype)


def attend_window(queries, keys, values, segment_ids, gate_here):
    tokens, width = queries.shape
    experts = width // HD
    blocks = tokens // CHUNK
    window = min(blocks, SEG_MOST // CHUNK + 1)
    gate_cols = jnp.transpose(gate_here).reshape(experts, tokens, 1)
    seg_cols = segment_ids.reshape(tokens, 1)
    seg_row = segment_ids.reshape(1, tokens)
    return pl.pallas_call(
        lambda *refs: attention_kernel(window, *refs),
        grid=(blocks,),
        in_specs=[
            pl.BlockSpec((CHUNK, width), lambda i: (i, 0)),
            pl.BlockSpec((tokens, HD), lambda i: (0, 0)),
            pl.BlockSpec((tokens, HD), lambda i: (0, 0)),
            pl.BlockSpec((CHUNK, 1), lambda i: (i, 0)),
            pl.BlockSpec((1, tokens), lambda i: (0, 0)),
            pl.BlockSpec((experts, CHUNK, 1), lambda i: (0, i, 0)),
        ],
        out_specs=pl.BlockSpec((CHUNK, width), lambda i: (i, 0)),
        out_shape=jax.ShapeDtypeStruct((tokens, width), jnp.bfloat16),
        cost_estimate=pl.CostEstimate(
            flops=4 * tokens * window * CHUNK * width,
            transcendentals=tokens * window * CHUNK * experts,
            bytes_accessed=2 * tokens * width * 2 + 2 * tokens * HD * 2,
        ),
    )(queries, keys, values, seg_cols, seg_row, gate_cols)


def local(
    hidden,
    norm_gain,
    router_weight,
    kv_weight,
    query_weight,
    out_weight,
    routes,
    segment_ids,
    page_table,
    kv_cache,
):
    device_index = lax.axis_index("tensor")
    token_count = routes.shape[0]
    normed = lax.all_gather(normalize(hidden, norm_gain), "tensor", axis=0, tiled=True)
    gates = gate_table(normed, router_weight, routes)
    positions = positions_of(segment_ids)
    kv_width = kv_weight.shape[1]
    block_count = kv_width // HD
    own_rows = project_kv(normed, kv_weight, positions, device_index * block_count)
    new_cache = write_pages(kv_cache, page_table, own_rows.reshape(page_table.shape[0], PAGE, kv_width))
    partner_rows = swapped(own_rows, "tensor", 0)
    leading_first = device_index % 2 == 0
    head_rows = jnp.where(
        leading_first,
        jnp.concatenate([own_rows, partner_rows], axis=1),
        jnp.concatenate([partner_rows, own_rows], axis=1),
    )
    local_heads = head_rows.shape[1] // (2 * HD)
    head_rows = head_rows.reshape(token_count, local_heads, 2, HD)
    pair_count = query_weight.shape[1] // HD
    local_experts = pair_count // local_heads
    scale_factor = HD ** (-0.5)
    queries = jnp.dot(normed, query_weight, preferred_element_type=jnp.float32)
    queries = queries.reshape(token_count, local_experts, HD)
    queries = (rotate(queries, positions) * scale_factor).astype(jnp.bfloat16)
    first_expert = (device_index * pair_count) % EA
    gate_here = lax.dynamic_slice_in_dim(gates, first_expert, local_experts, 1)
    flat = attend_window(
        queries.reshape(token_count, pair_count * HD),
        head_rows[:, 0, 0],
        head_rows[:, 0, 1],
        segment_ids,
        gate_here,
    )
    partial = jnp.dot(flat, out_weight, preferred_element_type=jnp.float32).astype(jnp.bfloat16)
    reduced = reduce_to_owner(partial, "tensor").astype(jnp.float32)
    attended_out = (hidden.astype(jnp.float32) + reduced).astype(jnp.bfloat16)
    return (attended_out, new_cache)


def solution(mesh):
    placed = (
        P(("dp", "tensor"), None),
        P(),
        P(),
        P(None, "tensor"),
        P(None, "tensor"),
        P("tensor", None),
        P("dp", None),
        P("dp"),
        P("dp"),
        P("dp", None, "tensor"),
    )
    return jax.shard_map(
        local,
        mesh=mesh,
        in_specs=placed,
        out_specs=(P(("dp", "tensor"), None), P("dp", None, "tensor")),
        check_vma=False,
    )
```

```python
import jax
import jax.numpy as jnp
from jax import lax
from jax.experimental import pallas as pl
from jax.experimental.pallas import tpu as pltpu
from jax.sharding import PartitionSpec as P

D = 2048
HD = 128
EA = 8
PAGE = 128
REDUCE_PARTS = 4
SEG_MOST = 512
CHUNK = 128


def swapped(array, axis, bit):
    return lax.ppermute(array, axis, [(i, i ^ 1 << bit) for i in range(lax.axis_size(axis))])


def normalize(hidden, norm_gain):
    values = hidden.astype(jnp.float32)
    factor = lax.rsqrt(jnp.mean(values * values, axis=-1, keepdims=True) + 1e-05)
    return (values * factor * norm_gain.astype(jnp.float32)).astype(jnp.bfloat16)


def gate_table(normed, router_weight, routes):
    logits = jnp.dot(normed, router_weight, preferred_element_type=jnp.float32)
    expert_ids = jnp.arange(router_weight.shape[1], dtype=jnp.int32)
    onehot = routes[:, :, None] == expert_ids[None, None, :]
    chosen = jnp.sum(jnp.where(onehot, logits[:, None, :], 0.0), axis=2)
    weights = jax.nn.softmax(chosen, axis=-1)
    return jnp.sum(jnp.where(onehot, weights[:, :, None], 0.0), axis=1)


def positions_of(segment_ids):
    index_row = jnp.arange(segment_ids.shape[0], dtype=jnp.int32)
    starts_here = jnp.concatenate([jnp.ones((1,), dtype=bool), segment_ids[1:] != segment_ids[:-1]])
    segment_start = lax.cummax(jnp.where(starts_here, index_row, 0), axis=0)
    return index_row - segment_start


def rotate(values, positions):
    half_width = values.shape[-1] // 2
    frequency = 10000.0 ** (-jnp.arange(half_width, dtype=jnp.float32) / half_width)
    angles = positions.astype(jnp.float32)[:, None] * frequency[None, :]
    angles = angles.reshape((values.shape[0],) + (1,) * (values.ndim - 2) + (half_width,))
    cosine = jnp.cos(angles)
    sine_part = jnp.sin(angles)
    leading = values[..., :half_width]
    trailing = values[..., half_width:]
    return jnp.concatenate(
        [leading * cosine - trailing * sine_part, trailing * cosine + leading * sine_part], axis=-1
    )


def project_kv(normed, weight, positions, first_block):
    projected = jnp.dot(normed, weight, preferred_element_type=jnp.float32)
    block_total = weight.shape[1] // HD
    blocks = projected.reshape(normed.shape[0], block_total, HD)
    block_index = first_block + jnp.arange(block_total, dtype=jnp.int32)
    turned = rotate(blocks, positions)
    chosen = jnp.where((block_index % 2 == 0)[None, :, None], turned, blocks)
    return chosen.astype(jnp.bfloat16).reshape(normed.shape[0], weight.shape[1])


def write_pages(kv_cache, page_table, rows):
    pages = jnp.arange(kv_cache.shape[0], dtype=jnp.int32)
    hit = page_table[None, :] == pages[:, None]
    placed = jnp.einsum(
        "pb,brc->prc", hit.astype(rows.dtype), rows, preferred_element_type=jnp.float32
    ).astype(kv_cache.dtype)
    return jnp.where(jnp.any(hit, axis=1)[:, None, None], placed, kv_cache)


def bit_orders(bits, parts):
    rest = list(range(1, bits))
    if not rest:
        return [[0]] * parts
    return [[0] + rest[j % len(rest):] + rest[:j % len(rest)] for j in range(parts)]


def reduce_to_owner(partial, axis):
    size = lax.axis_size(axis)
    bits = size.bit_length() - 1
    assert 1 << bits == size
    me = lax.axis_index(axis)
    rows, width = partial.shape
    block = rows // size
    parts = REDUCE_PARTS if width % REDUCE_PARTS == 0 else 1
    piece = width // parts
    outs = []
    for j, order in enumerate(bit_orders(bits, parts)):
        cols = partial[:, j * piece:(j + 1) * piece]
        cube = cols.reshape((2,) * bits + (block, piece))
        cube = jnp.transpose(cube, [bits - 1 - k for k in order] + [bits, bits + 1])
        current = cube.reshape(rows, piece)
        for k in order:
            half = current.shape[0] // 2
            mine = (me >> k) & 1
            keep = lax.dynamic_slice_in_dim(current, mine * half, half, 0)
            send = lax.dynamic_slice_in_dim(current, (1 - mine) * half, half, 0)
            got = lax.ppermute(send, axis, [(i, i ^ (1 << k)) for i in range(size)])
            current = (keep.astype(jnp.float32) + got.astype(jnp.float32)).astype(jnp.bfloat16)
        outs.append(current)
    return jnp.concatenate(outs, axis=1)


def attention_kernel(window, q_ref, k_ref, v_ref, qseg_ref, kseg_ref, gate_ref, out_ref):
    chunk = pl.program_id(0)
    blocks = pl.num_programs(0)
    start_block = jnp.clip(chunk - (window - 1), 0, blocks - window)
    start = pl.multiple_of(start_block * CHUNK, CHUNK)
    span = window * CHUNK
    keys = k_ref[pl.ds(start, span), :]
    values = v_ref[pl.ds(start, span), :]
    key_seg = kseg_ref[:, pl.ds(start, span)]
    query_seg = qseg_ref[...]
    query_index = chunk * CHUNK + lax.broadcasted_iota(jnp.int32, (CHUNK, span), 0)
    key_index = start + lax.broadcasted_iota(jnp.int32, (CHUNK, span), 1)
    allowed = (query_seg == key_seg) & (key_index <= query_index)
    experts = gate_ref.shape[0]
    for e in range(experts):
        queries = q_ref[:, e * HD:(e + 1) * HD]
        scores = lax.dot_general(
            queries, keys, (((1,), (1,)), ((), ())), preferred_element_type=jnp.float32
        )
        scores = jnp.where(allowed, scores, -1e30)
        top = jnp.max(scores, axis=1, keepdims=True)
        raised = jnp.exp(scores - top)
        probabilities = (raised / jnp.sum(raised, axis=1, keepdims=True)).astype(jnp.bfloat16)
        attended = jnp.dot(probabilities, values, preferred_element_type=jnp.float32)
        out_ref[:, e * HD:(e + 1) * HD] = (attended * gate_ref[e]).astype(out_ref.dtype)


def attend_window(queries, keys, values, segment_ids, gate_here):
    tokens, width = queries.shape
    experts = width // HD
    blocks = tokens // CHUNK
    window = min(blocks, SEG_MOST // CHUNK + 1)
    gate_cols = jnp.transpose(gate_here).reshape(experts, tokens, 1)
    seg_cols = segment_ids.reshape(tokens, 1)
    seg_row = segment_ids.reshape(1, tokens)
    return pl.pallas_call(
        lambda *refs: attention_kernel(window, *refs),
        grid=(blocks,),
        in_specs=[
            pl.BlockSpec((CHUNK, width), lambda i: (i, 0)),
            pl.BlockSpec((tokens, HD), lambda i: (0, 0)),
            pl.BlockSpec((tokens, HD), lambda i: (0, 0)),
            pl.BlockSpec((CHUNK, 1), lambda i: (i, 0)),
            pl.BlockSpec((1, tokens), lambda i: (0, 0)),
            pl.BlockSpec((experts, CHUNK, 1), lambda i: (0, i, 0)),
        ],
        out_specs=pl.BlockSpec((CHUNK, width), lambda i: (i, 0)),
        out_shape=jax.ShapeDtypeStruct((tokens, width), jnp.bfloat16),
        cost_estimate=pl.CostEstimate(
            flops=4 * tokens * window * CHUNK * width,
            transcendentals=tokens * window * CHUNK * experts,
            bytes_accessed=2 * tokens * width * 2 + 2 * tokens * HD * 2,
        ),
    )(queries, keys, values, seg_cols, seg_row, gate_cols)


def gather_from_all(block, axis):
    size = lax.axis_size(axis)
    bits = size.bit_length() - 1
    assert 1 << bits == size
    me = lax.axis_index(axis)
    rows, width = block.shape
    parts = REDUCE_PARTS if width % REDUCE_PARTS == 0 else 1
    piece = width // parts
    outs = []
    for j, forward in enumerate(bit_orders(bits, parts)):
        order = forward[::-1]
        current = block[:, j * piece:(j + 1) * piece]
        for k in order:
            got = lax.ppermute(current, axis, [(i, i ^ (1 << k)) for i in range(size)])
            upper = ((me >> k) & 1) == 1
            current = jnp.concatenate(
                [jnp.where(upper, got, current), jnp.where(upper, current, got)], axis=0
            )
        cube = current.reshape((2,) * bits + (rows, piece))
        old_axis = {order[bits - 1 - a]: a for a in range(bits)}
        cube = jnp.transpose(cube, [old_axis[bits - 1 - a] for a in range(bits)] + [bits, bits + 1])
        outs.append(cube.reshape(size * rows, piece))
    return jnp.concatenate(outs, axis=1)


def local(
    hidden,
    norm_gain,
    router_weight,
    kv_weight,
    query_weight,
    out_weight,
    routes,
    segment_ids,
    page_table,
    kv_cache,
):
    device_index = lax.axis_index("tensor")
    token_count = routes.shape[0]
    normed = gather_from_all(normalize(hidden, norm_gain), "tensor")
    gates = gate_table(normed, router_weight, routes)
    positions = positions_of(segment_ids)
    kv_width = kv_weight.shape[1]
    block_count = kv_width // HD
    own_rows = project_kv(normed, kv_weight, positions, device_index * block_count)
    new_cache = write_pages(kv_cache, page_table, own_rows.reshape(page_table.shape[0], PAGE, kv_width))
    partner_rows = swapped(own_rows, "tensor", 0)
    leading_first = device_index % 2 == 0
    head_rows = jnp.where(
        leading_first,
        jnp.concatenate([own_rows, partner_rows], axis=1),
        jnp.concatenate([partner_rows, own_rows], axis=1),
    )
    local_heads = head_rows.shape[1] // (2 * HD)
    head_rows = head_rows.reshape(token_count, local_heads, 2, HD)
    pair_count = query_weight.shape[1] // HD
    local_experts = pair_count // local_heads
    scale_factor = HD ** (-0.5)
    queries = jnp.dot(normed, query_weight, preferred_element_type=jnp.float32)
    queries = queries.reshape(token_count, local_experts, HD)
    queries = (rotate(queries, positions) * scale_factor).astype(jnp.bfloat16)
    first_expert = (device_index * pair_count) % EA
    gate_here = lax.dynamic_slice_in_dim(gates, first_expert, local_experts, 1)
    flat = attend_window(
        queries.reshape(token_count, pair_count * HD),
        head_rows[:, 0, 0],
        head_rows[:, 0, 1],
        segment_ids,
        gate_here,
    )
    partial = jnp.dot(flat, out_weight, preferred_element_type=jnp.float32).astype(jnp.bfloat16)
    reduced = reduce_to_owner(partial, "tensor").astype(jnp.float32)
    attended_out = (hidden.astype(jnp.float32) + reduced).astype(jnp.bfloat16)
    return (attended_out, new_cache)


def solution(mesh):
    placed = (
        P(("dp", "tensor"), None),
        P(),
        P(),
        P(None, "tensor"),
        P(None, "tensor"),
        P("tensor", None),
        P("dp", None),
        P("dp"),
        P("dp"),
        P("dp", None, "tensor"),
    )
    return jax.shard_map(
        local,
        mesh=mesh,
        in_specs=placed,
        out_specs=(P(("dp", "tensor"), None), P("dp", None, "tensor")),
        check_vma=False,
    )
```

```python
import jax
import jax.numpy as jnp
from jax import lax
from jax.experimental import pallas as pl
from jax.experimental.pallas import tpu as pltpu
from jax.sharding import PartitionSpec as P

D = 2048
HD = 128
EA = 8
PAGE = 128
REDUCE_PARTS = 4
SEG_MOST = 512
CHUNK = 128


def swapped(array, axis, bit):
    return lax.ppermute(array, axis, [(i, i ^ 1 << bit) for i in range(lax.axis_size(axis))])


def normalize(hidden, norm_gain):
    values = hidden.astype(jnp.float32)
    factor = lax.rsqrt(jnp.mean(values * values, axis=-1, keepdims=True) + 1e-05)
    return (values * factor * norm_gain.astype(jnp.float32)).astype(jnp.bfloat16)


def gate_table(normed, router_weight, routes):
    logits = jnp.dot(normed, router_weight, preferred_element_type=jnp.float32)
    expert_ids = jnp.arange(router_weight.shape[1], dtype=jnp.int32)
    onehot = routes[:, :, None] == expert_ids[None, None, :]
    chosen = jnp.sum(jnp.where(onehot, logits[:, None, :], 0.0), axis=2)
    weights = jax.nn.softmax(chosen, axis=-1)
    return jnp.sum(jnp.where(onehot, weights[:, :, None], 0.0), axis=1)


def positions_of(segment_ids):
    index_row = jnp.arange(segment_ids.shape[0], dtype=jnp.int32)
    starts_here = jnp.concatenate([jnp.ones((1,), dtype=bool), segment_ids[1:] != segment_ids[:-1]])
    segment_start = lax.cummax(jnp.where(starts_here, index_row, 0), axis=0)
    return index_row - segment_start


def rotate(values, positions):
    half_width = values.shape[-1] // 2
    frequency = 10000.0 ** (-jnp.arange(half_width, dtype=jnp.float32) / half_width)
    angles = positions.astype(jnp.float32)[:, None] * frequency[None, :]
    angles = angles.reshape((values.shape[0],) + (1,) * (values.ndim - 2) + (half_width,))
    cosine = jnp.cos(angles)
    sine_part = jnp.sin(angles)
    leading = values[..., :half_width]
    trailing = values[..., half_width:]
    return jnp.concatenate(
        [leading * cosine - trailing * sine_part, trailing * cosine + leading * sine_part], axis=-1
    )


def project_kv(normed, weight, positions, first_block):
    projected = jnp.dot(normed, weight, preferred_element_type=jnp.float32)
    block_total = weight.shape[1] // HD
    blocks = projected.reshape(normed.shape[0], block_total, HD)
    block_index = first_block + jnp.arange(block_total, dtype=jnp.int32)
    turned = rotate(blocks, positions)
    chosen = jnp.where((block_index % 2 == 0)[None, :, None], turned, blocks)
    return chosen.astype(jnp.bfloat16).reshape(normed.shape[0], weight.shape[1])


def write_pages(kv_cache, page_table, rows):
    pages = jnp.arange(kv_cache.shape[0], dtype=jnp.int32)
    hit = page_table[None, :] == pages[:, None]
    placed = jnp.einsum(
        "pb,brc->prc", hit.astype(rows.dtype), rows, preferred_element_type=jnp.float32
    ).astype(kv_cache.dtype)
    return jnp.where(jnp.any(hit, axis=1)[:, None, None], placed, kv_cache)


def bit_orders(bits, parts):
    rest = list(range(1, bits))
    if not rest:
        return [[0]] * parts
    return [[0] + rest[j % len(rest):] + rest[:j % len(rest)] for j in range(parts)]


def reduce_to_owner(partial, axis):
    size = lax.axis_size(axis)
    bits = size.bit_length() - 1
    assert 1 << bits == size
    me = lax.axis_index(axis)
    rows, width = partial.shape
    block = rows // size
    parts = REDUCE_PARTS if width % REDUCE_PARTS == 0 else 1
    piece = width // parts
    outs = []
    for j, order in enumerate(bit_orders(bits, parts)):
        cols = partial[:, j * piece:(j + 1) * piece]
        cube = cols.reshape((2,) * bits + (block, piece))
        cube = jnp.transpose(cube, [bits - 1 - k for k in order] + [bits, bits + 1])
        current = cube.reshape(rows, piece)
        for k in order:
            half = current.shape[0] // 2
            mine = (me >> k) & 1
            keep = lax.dynamic_slice_in_dim(current, mine * half, half, 0)
            send = lax.dynamic_slice_in_dim(current, (1 - mine) * half, half, 0)
            got = lax.ppermute(send, axis, [(i, i ^ (1 << k)) for i in range(size)])
            current = (keep.astype(jnp.float32) + got.astype(jnp.float32)).astype(jnp.bfloat16)
        outs.append(current)
    return jnp.concatenate(outs, axis=1)


def attention_kernel(window, q_ref, cos_ref, sin_ref, k_ref, v_ref, qseg_ref, kseg_ref, gate_ref, out_ref):
    chunk = pl.program_id(0)
    blocks = pl.num_programs(0)
    start_block = jnp.clip(chunk - (window - 1), 0, blocks - window)
    start = pl.multiple_of(start_block * CHUNK, CHUNK)
    span = window * CHUNK
    keys = k_ref[pl.ds(start, span), :]
    values = v_ref[pl.ds(start, span), :]
    key_seg = kseg_ref[:, pl.ds(start, span)]
    query_seg = qseg_ref[...]
    query_index = chunk * CHUNK + lax.broadcasted_iota(jnp.int32, (CHUNK, span), 0)
    key_index = start + lax.broadcasted_iota(jnp.int32, (CHUNK, span), 1)
    allowed = (query_seg == key_seg) & (key_index <= query_index)
    cosine = cos_ref[...]
    sine_part = sin_ref[...]
    scale_factor = HD ** (-0.5)
    experts = gate_ref.shape[1]
    for e in range(experts):
        raw = q_ref[:, e * HD:(e + 1) * HD]
        turned = raw * cosine + pltpu.roll(raw, HD // 2, 1) * sine_part
        queries = (turned * scale_factor).astype(jnp.bfloat16)
        scores = lax.dot_general(
            queries, keys, (((1,), (1,)), ((), ())), preferred_element_type=jnp.float32
        )
        scores = jnp.where(allowed, scores, -1e30)
        top = jnp.max(scores, axis=1, keepdims=True)
        raised = jnp.exp(scores - top)
        probabilities = (raised / jnp.sum(raised, axis=1, keepdims=True)).astype(jnp.bfloat16)
        attended = jnp.dot(probabilities, values, preferred_element_type=jnp.float32)
        out_ref[:, e * HD:(e + 1) * HD] = (attended * gate_ref[:, e:e + 1]).astype(out_ref.dtype)


def rope_tables(positions):
    half_width = HD // 2
    frequency = 10000.0 ** (-jnp.arange(half_width, dtype=jnp.float32) / half_width)
    angles = positions.astype(jnp.float32)[:, None] * frequency[None, :]
    cosine = jnp.cos(angles)
    sine_part = jnp.sin(angles)
    return (
        jnp.concatenate([cosine, cosine], axis=1),
        jnp.concatenate([-sine_part, sine_part], axis=1),
    )


def attend_window(raw_queries, positions, keys, values, segment_ids, gate_here):
    tokens, width = raw_queries.shape
    experts = width // HD
    blocks = tokens // CHUNK
    window = min(blocks, SEG_MOST // CHUNK + 1)
    cosine, sine_part = rope_tables(positions)
    seg_cols = segment_ids.reshape(tokens, 1)
    seg_row = segment_ids.reshape(1, tokens)
    return pl.pallas_call(
        lambda *refs: attention_kernel(window, *refs),
        grid=(blocks,),
        in_specs=[
            pl.BlockSpec((CHUNK, width), lambda i: (i, 0)),
            pl.BlockSpec((CHUNK, HD), lambda i: (i, 0)),
            pl.BlockSpec((CHUNK, HD), lambda i: (i, 0)),
            pl.BlockSpec((tokens, HD), lambda i: (0, 0)),
            pl.BlockSpec((tokens, HD), lambda i: (0, 0)),
            pl.BlockSpec((CHUNK, 1), lambda i: (i, 0)),
            pl.BlockSpec((1, tokens), lambda i: (0, 0)),
            pl.BlockSpec((CHUNK, experts), lambda i: (i, 0)),
        ],
        out_specs=pl.BlockSpec((CHUNK, width), lambda i: (i, 0)),
        out_shape=jax.ShapeDtypeStruct((tokens, width), jnp.bfloat16),
        cost_estimate=pl.CostEstimate(
            flops=4 * tokens * window * CHUNK * width,
            transcendentals=tokens * window * CHUNK * experts,
            bytes_accessed=tokens * width * 6 + 2 * tokens * HD * 2 + 2 * tokens * HD * 4,
        ),
    )(raw_queries, cosine, sine_part, keys, values, seg_cols, seg_row, gate_here)


def gather_from_all(block, axis):
    size = lax.axis_size(axis)
    bits = size.bit_length() - 1
    assert 1 << bits == size
    me = lax.axis_index(axis)
    rows, width = block.shape
    parts = REDUCE_PARTS if width % REDUCE_PARTS == 0 else 1
    piece = width // parts
    outs = []
    for j, forward in enumerate(bit_orders(bits, parts)):
        order = forward[::-1]
        current = block[:, j * piece:(j + 1) * piece]
        for k in order:
            got = lax.ppermute(current, axis, [(i, i ^ (1 << k)) for i in range(size)])
            upper = ((me >> k) & 1) == 1
            current = jnp.concatenate(
                [jnp.where(upper, got, current), jnp.where(upper, current, got)], axis=0
            )
        cube = current.reshape((2,) * bits + (rows, piece))
        old_axis = {order[bits - 1 - a]: a for a in range(bits)}
        cube = jnp.transpose(cube, [old_axis[bits - 1 - a] for a in range(bits)] + [bits, bits + 1])
        outs.append(cube.reshape(size * rows, piece))
    return jnp.concatenate(outs, axis=1)


def local(
    hidden,
    norm_gain,
    router_weight,
    kv_weight,
    query_weight,
    out_weight,
    routes,
    segment_ids,
    page_table,
    kv_cache,
):
    device_index = lax.axis_index("tensor")
    token_count = routes.shape[0]
    normed = gather_from_all(normalize(hidden, norm_gain), "tensor")
    gates = gate_table(normed, router_weight, routes)
    positions = positions_of(segment_ids)
    kv_width = kv_weight.shape[1]
    block_count = kv_width // HD
    own_rows = project_kv(normed, kv_weight, positions, device_index * block_count)
    new_cache = write_pages(kv_cache, page_table, own_rows.reshape(page_table.shape[0], PAGE, kv_width))
    partner_rows = swapped(own_rows, "tensor", 0)
    leading_first = device_index % 2 == 0
    key_rows = jnp.where(leading_first, own_rows, partner_rows)
    value_rows = jnp.where(leading_first, partner_rows, own_rows)
    pair_count = query_weight.shape[1] // HD
    raw_queries = jnp.dot(normed, query_weight, preferred_element_type=jnp.float32)
    first_expert = (device_index * pair_count) % EA
    gate_here = lax.dynamic_slice_in_dim(gates, first_expert, pair_count, 1)
    flat = attend_window(raw_queries, positions, key_rows, value_rows, segment_ids, gate_here)
    partial = jnp.dot(flat, out_weight, preferred_element_type=jnp.float32).astype(jnp.bfloat16)
    reduced = reduce_to_owner(partial, "tensor").astype(jnp.float32)
    attended_out = (hidden.astype(jnp.float32) + reduced).astype(jnp.bfloat16)
    return (attended_out, new_cache)


def solution(mesh):
    placed = (
        P(("dp", "tensor"), None),
        P(),
        P(),
        P(None, "tensor"),
        P(None, "tensor"),
        P("tensor", None),
        P("dp", None),
        P("dp"),
        P("dp"),
        P("dp", None, "tensor"),
    )
    return jax.shard_map(
        local,
        mesh=mesh,
        in_specs=placed,
        out_specs=(P(("dp", "tensor"), None), P("dp", None, "tensor")),
        check_vma=False,
    )
```

```python
import jax
import jax.numpy as jnp
from jax import lax
from jax.experimental import pallas as pl
from jax.experimental.pallas import tpu as pltpu
from jax.sharding import PartitionSpec as P

D = 2048
HD = 128
EA = 8
PAGE = 128
REDUCE_PARTS = 4
SEG_MOST = 512
CHUNK = 128


def swapped(array, axis, bit):
    return lax.ppermute(array, axis, [(i, i ^ 1 << bit) for i in range(lax.axis_size(axis))])


def normalize(hidden, norm_gain):
    values = hidden.astype(jnp.float32)
    factor = lax.rsqrt(jnp.mean(values * values, axis=-1, keepdims=True) + 1e-05)
    return (values * factor * norm_gain.astype(jnp.float32)).astype(jnp.bfloat16)


def gate_table(normed, router_weight, routes):
    logits = jnp.dot(normed, router_weight, preferred_element_type=jnp.float32)
    expert_ids = jnp.arange(router_weight.shape[1], dtype=jnp.int32)
    onehot = routes[:, :, None] == expert_ids[None, None, :]
    chosen = jnp.sum(jnp.where(onehot, logits[:, None, :], 0.0), axis=2)
    weights = jax.nn.softmax(chosen, axis=-1)
    return jnp.sum(jnp.where(onehot, weights[:, :, None], 0.0), axis=1)


def positions_of(segment_ids):
    index_row = jnp.arange(segment_ids.shape[0], dtype=jnp.int32)
    starts_here = jnp.concatenate([jnp.ones((1,), dtype=bool), segment_ids[1:] != segment_ids[:-1]])
    segment_start = lax.cummax(jnp.where(starts_here, index_row, 0), axis=0)
    return index_row - segment_start


def rotate(values, positions):
    half_width = values.shape[-1] // 2
    frequency = 10000.0 ** (-jnp.arange(half_width, dtype=jnp.float32) / half_width)
    angles = positions.astype(jnp.float32)[:, None] * frequency[None, :]
    angles = angles.reshape((values.shape[0],) + (1,) * (values.ndim - 2) + (half_width,))
    cosine = jnp.cos(angles)
    sine_part = jnp.sin(angles)
    leading = values[..., :half_width]
    trailing = values[..., half_width:]
    return jnp.concatenate(
        [leading * cosine - trailing * sine_part, trailing * cosine + leading * sine_part], axis=-1
    )


def project_kv(normed, weight, positions, first_block):
    projected = jnp.dot(normed, weight, preferred_element_type=jnp.float32)
    block_total = weight.shape[1] // HD
    blocks = projected.reshape(normed.shape[0], block_total, HD)
    block_index = first_block + jnp.arange(block_total, dtype=jnp.int32)
    turned = rotate(blocks, positions)
    chosen = jnp.where((block_index % 2 == 0)[None, :, None], turned, blocks)
    return chosen.astype(jnp.bfloat16).reshape(normed.shape[0], weight.shape[1])


def write_pages(kv_cache, page_table, rows):
    pages = jnp.arange(kv_cache.shape[0], dtype=jnp.int32)
    hit = page_table[None, :] == pages[:, None]
    placed = jnp.einsum(
        "pb,brc->prc", hit.astype(rows.dtype), rows, preferred_element_type=jnp.float32
    ).astype(kv_cache.dtype)
    return jnp.where(jnp.any(hit, axis=1)[:, None, None], placed, kv_cache)


def bit_orders(bits, parts):
    rest = list(range(1, bits))
    return [rest[j % len(rest):] + rest[:j % len(rest)] for j in range(parts)]


def reduce_to_owner(partial, axis):
    size = lax.axis_size(axis)
    bits = size.bit_length() - 1
    assert 1 << bits == size and bits >= 1
    me = lax.axis_index(axis)
    rows, width = partial.shape
    block = rows // size
    low = me & 1
    paired = partial.reshape(size // 2, 2, block, width)
    keep = lax.dynamic_index_in_dim(paired, low, 1, keepdims=False)
    send = lax.dynamic_index_in_dim(paired, 1 - low, 1, keepdims=False)
    got = lax.ppermute(send, axis, [(i, i ^ 1) for i in range(size)])
    halved = (keep.astype(jnp.float32) + got.astype(jnp.float32)).astype(jnp.bfloat16)
    if bits == 1:
        return halved.reshape(block, width)
    parts = REDUCE_PARTS if width % REDUCE_PARTS == 0 else 1
    piece = width // parts
    outs = []
    for j, order in enumerate(bit_orders(bits, parts)):
        cols = halved[:, :, j * piece:(j + 1) * piece]
        cube = cols.reshape((2,) * (bits - 1) + (block, piece))
        cube = jnp.transpose(cube, [bits - 1 - k for k in order] + [bits - 1, bits])
        current = cube.reshape(rows // 2, piece)
        for k in order:
            half = current.shape[0] // 2
            mine = (me >> k) & 1
            keep = lax.dynamic_slice_in_dim(current, mine * half, half, 0)
            send = lax.dynamic_slice_in_dim(current, (1 - mine) * half, half, 0)
            got = lax.ppermute(send, axis, [(i, i ^ (1 << k)) for i in range(size)])
            current = (keep.astype(jnp.float32) + got.astype(jnp.float32)).astype(jnp.bfloat16)
        outs.append(current)
    return jnp.concatenate(outs, axis=1)


def attention_kernel(window, q_ref, cos_ref, sin_ref, k_ref, v_ref, qseg_ref, kseg_ref, gate_ref, out_ref):
    chunk = pl.program_id(0)
    blocks = pl.num_programs(0)
    start_block = jnp.clip(chunk - (window - 1), 0, blocks - window)
    start = pl.multiple_of(start_block * CHUNK, CHUNK)
    span = window * CHUNK
    keys = k_ref[pl.ds(start, span), :]
    values = v_ref[pl.ds(start, span), :]
    key_seg = kseg_ref[:, pl.ds(start, span)]
    query_seg = qseg_ref[...]
    query_index = chunk * CHUNK + lax.broadcasted_iota(jnp.int32, (CHUNK, span), 0)
    key_index = start + lax.broadcasted_iota(jnp.int32, (CHUNK, span), 1)
    allowed = (query_seg == key_seg) & (key_index <= query_index)
    cosine = cos_ref[...]
    sine_part = sin_ref[...]
    scale_factor = HD ** (-0.5)
    experts = gate_ref.shape[1]
    for e in range(experts):
        raw = q_ref[:, e * HD:(e + 1) * HD]
        turned = raw * cosine + pltpu.roll(raw, HD // 2, 1) * sine_part
        queries = (turned * scale_factor).astype(jnp.bfloat16)
        scores = lax.dot_general(
            queries, keys, (((1,), (1,)), ((), ())), preferred_element_type=jnp.float32
        )
        scores = jnp.where(allowed, scores, -1e30)
        top = jnp.max(scores, axis=1, keepdims=True)
        raised = jnp.exp(scores - top)
        probabilities = (raised / jnp.sum(raised, axis=1, keepdims=True)).astype(jnp.bfloat16)
        attended = jnp.dot(probabilities, values, preferred_element_type=jnp.float32)
        out_ref[:, e * HD:(e + 1) * HD] = (attended * gate_ref[:, e:e + 1]).astype(out_ref.dtype)


def rope_tables(positions):
    half_width = HD // 2
    frequency = 10000.0 ** (-jnp.arange(half_width, dtype=jnp.float32) / half_width)
    angles = positions.astype(jnp.float32)[:, None] * frequency[None, :]
    cosine = jnp.cos(angles)
    sine_part = jnp.sin(angles)
    return (
        jnp.concatenate([cosine, cosine], axis=1),
        jnp.concatenate([-sine_part, sine_part], axis=1),
    )


def attend_window(raw_queries, positions, keys, values, segment_ids, gate_here):
    tokens, width = raw_queries.shape
    experts = width // HD
    blocks = tokens // CHUNK
    window = min(blocks, SEG_MOST // CHUNK + 1)
    cosine, sine_part = rope_tables(positions)
    seg_cols = segment_ids.reshape(tokens, 1)
    seg_row = segment_ids.reshape(1, tokens)
    return pl.pallas_call(
        lambda *refs: attention_kernel(window, *refs),
        grid=(blocks,),
        in_specs=[
            pl.BlockSpec((CHUNK, width), lambda i: (i, 0)),
            pl.BlockSpec((CHUNK, HD), lambda i: (i, 0)),
            pl.BlockSpec((CHUNK, HD), lambda i: (i, 0)),
            pl.BlockSpec((tokens, HD), lambda i: (0, 0)),
            pl.BlockSpec((tokens, HD), lambda i: (0, 0)),
            pl.BlockSpec((CHUNK, 1), lambda i: (i, 0)),
            pl.BlockSpec((1, tokens), lambda i: (0, 0)),
            pl.BlockSpec((CHUNK, experts), lambda i: (i, 0)),
        ],
        out_specs=pl.BlockSpec((CHUNK, width), lambda i: (i, 0)),
        out_shape=jax.ShapeDtypeStruct((tokens, width), jnp.bfloat16),
        cost_estimate=pl.CostEstimate(
            flops=4 * tokens * window * CHUNK * width,
            transcendentals=tokens * window * CHUNK * experts,
            bytes_accessed=tokens * width * 6 + 2 * tokens * HD * 2 + 2 * tokens * HD * 4,
        ),
    )(raw_queries, cosine, sine_part, keys, values, seg_cols, seg_row, gate_here)


def gather_from_all(block, axis):
    size = lax.axis_size(axis)
    bits = size.bit_length() - 1
    assert 1 << bits == size and bits >= 1
    me = lax.axis_index(axis)
    rows, width = block.shape
    if bits > 1:
        parts = REDUCE_PARTS if width % REDUCE_PARTS == 0 else 1
        piece = width // parts
        outs = []
        for j, forward in enumerate(bit_orders(bits, parts)):
            order = forward[::-1]
            current = block[:, j * piece:(j + 1) * piece]
            for k in order:
                got = lax.ppermute(current, axis, [(i, i ^ (1 << k)) for i in range(size)])
                upper = ((me >> k) & 1) == 1
                current = jnp.concatenate(
                    [jnp.where(upper, got, current), jnp.where(upper, current, got)], axis=0
                )
            cube = current.reshape((2,) * (bits - 1) + (rows, piece))
            old_axis = {order[bits - 2 - a]: a for a in range(bits - 1)}
            cube = jnp.transpose(
                cube, [old_axis[bits - 1 - a] for a in range(bits - 1)] + [bits - 1, bits]
            )
            outs.append(cube.reshape(size // 2 * rows, piece))
        block = jnp.concatenate(outs, axis=1)
    got = lax.ppermute(block, axis, [(i, i ^ 1) for i in range(size)])
    upper = (me & 1) == 1
    lower_rows = jnp.where(upper, got, block).reshape(size // 2, 1, rows, width)
    upper_rows = jnp.where(upper, block, got).reshape(size // 2, 1, rows, width)
    return jnp.concatenate([lower_rows, upper_rows], axis=1).reshape(size * rows, width)


def local(
    hidden,
    norm_gain,
    router_weight,
    kv_weight,
    query_weight,
    out_weight,
    routes,
    segment_ids,
    page_table,
    kv_cache,
):
    device_index = lax.axis_index("tensor")
    token_count = routes.shape[0]
    normed = gather_from_all(normalize(hidden, norm_gain), "tensor")
    gates = gate_table(normed, router_weight, routes)
    positions = positions_of(segment_ids)
    kv_width = kv_weight.shape[1]
    block_count = kv_width // HD
    own_rows = project_kv(normed, kv_weight, positions, device_index * block_count)
    new_cache = write_pages(kv_cache, page_table, own_rows.reshape(page_table.shape[0], PAGE, kv_width))
    partner_rows = swapped(own_rows, "tensor", 0)
    leading_first = device_index % 2 == 0
    key_rows = jnp.where(leading_first, own_rows, partner_rows)
    value_rows = jnp.where(leading_first, partner_rows, own_rows)
    pair_count = query_weight.shape[1] // HD
    raw_queries = jnp.dot(normed, query_weight, preferred_element_type=jnp.float32)
    first_expert = (device_index * pair_count) % EA
    gate_here = lax.dynamic_slice_in_dim(gates, first_expert, pair_count, 1)
    flat = attend_window(raw_queries, positions, key_rows, value_rows, segment_ids, gate_here)
    partial = jnp.dot(flat, out_weight, preferred_element_type=jnp.float32).astype(jnp.bfloat16)
    reduced = reduce_to_owner(partial, "tensor").astype(jnp.float32)
    attended_out = (hidden.astype(jnp.float32) + reduced).astype(jnp.bfloat16)
    return (attended_out, new_cache)


def solution(mesh):
    placed = (
        P(("dp", "tensor"), None),
        P(),
        P(),
        P(None, "tensor"),
        P(None, "tensor"),
        P("tensor", None),
        P("dp", None),
        P("dp"),
        P("dp"),
        P("dp", None, "tensor"),
    )
    return jax.shard_map(
        local,
        mesh=mesh,
        in_specs=placed,
        out_specs=(P(("dp", "tensor"), None), P("dp", None, "tensor")),
        check_vma=False,
    )
```

```python
import jax
import jax.numpy as jnp
from jax import lax
from jax.experimental import pallas as pl
from jax.experimental.pallas import tpu as pltpu
from jax.sharding import PartitionSpec as P

D = 2048
HD = 128
EA = 8
PAGE = 128
REDUCE_PARTS = 4
SEG_MOST = 512
CHUNK = 128


def swapped(array, axis, bit):
    return lax.ppermute(array, axis, [(i, i ^ 1 << bit) for i in range(lax.axis_size(axis))])


def normalize(hidden, norm_gain):
    values = hidden.astype(jnp.float32)
    factor = lax.rsqrt(jnp.mean(values * values, axis=-1, keepdims=True) + 1e-05)
    return (values * factor * norm_gain.astype(jnp.float32)).astype(jnp.bfloat16)


def gate_table(normed, router_weight, routes):
    logits = jnp.dot(normed, router_weight, preferred_element_type=jnp.float32)
    expert_ids = jnp.arange(router_weight.shape[1], dtype=jnp.int32)
    onehot = routes[:, :, None] == expert_ids[None, None, :]
    chosen = jnp.sum(jnp.where(onehot, logits[:, None, :], 0.0), axis=2)
    weights = jax.nn.softmax(chosen, axis=-1)
    return jnp.sum(jnp.where(onehot, weights[:, :, None], 0.0), axis=1)


def positions_of(segment_ids):
    index_row = jnp.arange(segment_ids.shape[0], dtype=jnp.int32)
    starts_here = jnp.concatenate([jnp.ones((1,), dtype=bool), segment_ids[1:] != segment_ids[:-1]])
    segment_start = lax.cummax(jnp.where(starts_here, index_row, 0), axis=0)
    return index_row - segment_start


def rotate(values, positions):
    half_width = values.shape[-1] // 2
    frequency = 10000.0 ** (-jnp.arange(half_width, dtype=jnp.float32) / half_width)
    angles = positions.astype(jnp.float32)[:, None] * frequency[None, :]
    angles = angles.reshape((values.shape[0],) + (1,) * (values.ndim - 2) + (half_width,))
    cosine = jnp.cos(angles)
    sine_part = jnp.sin(angles)
    leading = values[..., :half_width]
    trailing = values[..., half_width:]
    return jnp.concatenate(
        [leading * cosine - trailing * sine_part, trailing * cosine + leading * sine_part], axis=-1
    )


def project_kv(normed, weight, positions, first_block):
    projected = jnp.dot(normed, weight, preferred_element_type=jnp.float32)
    block_total = weight.shape[1] // HD
    blocks = projected.reshape(normed.shape[0], block_total, HD)
    block_index = first_block + jnp.arange(block_total, dtype=jnp.int32)
    turned = rotate(blocks, positions)
    chosen = jnp.where((block_index % 2 == 0)[None, :, None], turned, blocks)
    return chosen.astype(jnp.bfloat16).reshape(normed.shape[0], weight.shape[1])


def write_pages(kv_cache, page_table, rows):
    pages = jnp.arange(kv_cache.shape[0], dtype=jnp.int32)
    hit = page_table[None, :] == pages[:, None]
    placed = jnp.einsum(
        "pb,brc->prc", hit.astype(rows.dtype), rows, preferred_element_type=jnp.float32
    ).astype(kv_cache.dtype)
    return jnp.where(jnp.any(hit, axis=1)[:, None, None], placed, kv_cache)


def bit_orders(bits, parts):
    rest = list(range(1, bits))
    if not rest:
        return [[0]] * parts
    return [[0] + rest[j % len(rest):] + rest[:j % len(rest)] for j in range(parts)]


def reduce_to_owner(partial, axis):
    size = lax.axis_size(axis)
    bits = size.bit_length() - 1
    assert 1 << bits == size
    me = lax.axis_index(axis)
    rows, width = partial.shape
    block = rows // size
    parts = REDUCE_PARTS if width % REDUCE_PARTS == 0 else 1
    piece = width // parts
    outs = []
    for j, order in enumerate(bit_orders(bits, parts)):
        cols = partial[:, j * piece:(j + 1) * piece]
        cube = cols.reshape((2,) * bits + (block, piece))
        cube = jnp.transpose(cube, [bits - 1 - k for k in order] + [bits, bits + 1])
        current = cube.reshape(rows, piece)
        for k in order:
            half = current.shape[0] // 2
            mine = (me >> k) & 1
            keep = lax.dynamic_slice_in_dim(current, mine * half, half, 0)
            send = lax.dynamic_slice_in_dim(current, (1 - mine) * half, half, 0)
            got = lax.ppermute(send, axis, [(i, i ^ (1 << k)) for i in range(size)])
            current = (keep.astype(jnp.float32) + got.astype(jnp.float32)).astype(jnp.bfloat16)
        outs.append(current)
    return jnp.concatenate(outs, axis=1)


def attention_kernel(window, q_ref, cos_ref, sin_ref, k_ref, v_ref, qseg_ref, kseg_ref, gate_ref, out_ref):
    chunk = pl.program_id(0)
    blocks = pl.num_programs(0)
    start_block = jnp.clip(chunk - (window - 1), 0, blocks - window)
    start = pl.multiple_of(start_block * CHUNK, CHUNK)
    span = window * CHUNK
    keys = k_ref[:, pl.ds(start, span)]
    values = v_ref[pl.ds(start, span), :]
    key_seg = kseg_ref[:, pl.ds(start, span)]
    query_seg = qseg_ref[...]
    query_index = chunk * CHUNK + lax.broadcasted_iota(jnp.int32, (CHUNK, span), 0)
    key_index = start + lax.broadcasted_iota(jnp.int32, (CHUNK, span), 1)
    allowed = (query_seg == key_seg) & (key_index <= query_index)
    cosine = cos_ref[...]
    sine_part = sin_ref[...]
    scale_factor = HD ** (-0.5)
    experts = gate_ref.shape[1]
    for e in range(experts):
        raw = q_ref[:, e * HD:(e + 1) * HD]
        turned = raw * cosine + pltpu.roll(raw, HD // 2, 1) * sine_part
        queries = (turned * scale_factor).astype(jnp.bfloat16)
        scores = jnp.dot(queries, keys, preferred_element_type=jnp.float32)
        scores = jnp.where(allowed, scores, -1e30)
        top = jnp.max(scores, axis=1, keepdims=True)
        raised = jnp.exp(scores - top)
        inverse = 1.0 / jnp.sum(raised, axis=1, keepdims=True)
        probabilities = (raised * inverse).astype(jnp.bfloat16)
        attended = jnp.dot(probabilities, values, preferred_element_type=jnp.float32)
        out_ref[:, e * HD:(e + 1) * HD] = (attended * gate_ref[:, e:e + 1]).astype(out_ref.dtype)


def rope_tables(positions):
    half_width = HD // 2
    frequency = 10000.0 ** (-jnp.arange(half_width, dtype=jnp.float32) / half_width)
    angles = positions.astype(jnp.float32)[:, None] * frequency[None, :]
    cosine = jnp.cos(angles)
    sine_part = jnp.sin(angles)
    return (
        jnp.concatenate([cosine, cosine], axis=1),
        jnp.concatenate([-sine_part, sine_part], axis=1),
    )


def attend_window(raw_queries, positions, keys, values, segment_ids, gate_here):
    tokens, width = raw_queries.shape
    experts = width // HD
    blocks = tokens // CHUNK
    window = min(blocks, SEG_MOST // CHUNK + 1)
    cosine, sine_part = rope_tables(positions)
    seg_cols = segment_ids.reshape(tokens, 1)
    seg_row = segment_ids.reshape(1, tokens)
    return pl.pallas_call(
        lambda *refs: attention_kernel(window, *refs),
        grid=(blocks,),
        in_specs=[
            pl.BlockSpec((CHUNK, width), lambda i: (i, 0)),
            pl.BlockSpec((CHUNK, HD), lambda i: (i, 0)),
            pl.BlockSpec((CHUNK, HD), lambda i: (i, 0)),
            pl.BlockSpec((HD, tokens), lambda i: (0, 0)),
            pl.BlockSpec((tokens, HD), lambda i: (0, 0)),
            pl.BlockSpec((CHUNK, 1), lambda i: (i, 0)),
            pl.BlockSpec((1, tokens), lambda i: (0, 0)),
            pl.BlockSpec((CHUNK, experts), lambda i: (i, 0)),
        ],
        out_specs=pl.BlockSpec((CHUNK, width), lambda i: (i, 0)),
        out_shape=jax.ShapeDtypeStruct((tokens, width), jnp.bfloat16),
        cost_estimate=pl.CostEstimate(
            flops=4 * tokens * window * CHUNK * width,
            transcendentals=tokens * window * CHUNK * experts,
            bytes_accessed=tokens * width * 6 + 2 * tokens * HD * 2 + 2 * tokens * HD * 4,
        ),
    )(raw_queries, cosine, sine_part, jnp.transpose(keys), values, seg_cols, seg_row, gate_here)


def gather_from_all(block, axis):
    size = lax.axis_size(axis)
    bits = size.bit_length() - 1
    assert 1 << bits == size
    me = lax.axis_index(axis)
    rows, width = block.shape
    parts = REDUCE_PARTS if width % REDUCE_PARTS == 0 else 1
    piece = width // parts
    outs = []
    for j, forward in enumerate(bit_orders(bits, parts)):
        order = forward[::-1]
        current = block[:, j * piece:(j + 1) * piece]
        for k in order:
            got = lax.ppermute(current, axis, [(i, i ^ (1 << k)) for i in range(size)])
            upper = ((me >> k) & 1) == 1
            current = jnp.concatenate(
                [jnp.where(upper, got, current), jnp.where(upper, current, got)], axis=0
            )
        cube = current.reshape((2,) * bits + (rows, piece))
        old_axis = {order[bits - 1 - a]: a for a in range(bits)}
        cube = jnp.transpose(cube, [old_axis[bits - 1 - a] for a in range(bits)] + [bits, bits + 1])
        outs.append(cube.reshape(size * rows, piece))
    return jnp.concatenate(outs, axis=1)


def local(
    hidden,
    norm_gain,
    router_weight,
    kv_weight,
    query_weight,
    out_weight,
    routes,
    segment_ids,
    page_table,
    kv_cache,
):
    device_index = lax.axis_index("tensor")
    token_count = routes.shape[0]
    normed = gather_from_all(normalize(hidden, norm_gain), "tensor")
    gates = gate_table(normed, router_weight, routes)
    positions = positions_of(segment_ids)
    kv_width = kv_weight.shape[1]
    block_count = kv_width // HD
    own_rows = project_kv(normed, kv_weight, positions, device_index * block_count)
    new_cache = write_pages(kv_cache, page_table, own_rows.reshape(page_table.shape[0], PAGE, kv_width))
    partner_rows = swapped(own_rows, "tensor", 0)
    leading_first = device_index % 2 == 0
    key_rows = jnp.where(leading_first, own_rows, partner_rows)
    value_rows = jnp.where(leading_first, partner_rows, own_rows)
    pair_count = query_weight.shape[1] // HD
    raw_queries = jnp.dot(normed, query_weight, preferred_element_type=jnp.float32)
    first_expert = (device_index * pair_count) % EA
    gate_here = lax.dynamic_slice_in_dim(gates, first_expert, pair_count, 1)
    flat = attend_window(raw_queries, positions, key_rows, value_rows, segment_ids, gate_here)
    partial = jnp.dot(flat, out_weight, preferred_element_type=jnp.float32).astype(jnp.bfloat16)
    reduced = reduce_to_owner(partial, "tensor").astype(jnp.float32)
    attended_out = (hidden.astype(jnp.float32) + reduced).astype(jnp.bfloat16)
    return (attended_out, new_cache)


def solution(mesh):
    placed = (
        P(("dp", "tensor"), None),
        P(),
        P(),
        P(None, "tensor"),
        P(None, "tensor"),
        P("tensor", None),
        P("dp", None),
        P("dp"),
        P("dp"),
        P("dp", None, "tensor"),
    )
    return jax.shard_map(
        local,
        mesh=mesh,
        in_specs=placed,
        out_specs=(P(("dp", "tensor"), None), P("dp", None, "tensor")),
        check_vma=False,
    )
```

```python
import jax
import jax.numpy as jnp
from jax import lax
from jax.experimental import pallas as pl
from jax.experimental.pallas import tpu as pltpu
from jax.sharding import PartitionSpec as P

D = 2048
HD = 128
EA = 8
PAGE = 128
REDUCE_PARTS = 4
SEG_MOST = 512
CHUNK = 256


def swapped(array, axis, bit):
    return lax.ppermute(array, axis, [(i, i ^ 1 << bit) for i in range(lax.axis_size(axis))])


def normalize(hidden, norm_gain):
    values = hidden.astype(jnp.float32)
    factor = lax.rsqrt(jnp.mean(values * values, axis=-1, keepdims=True) + 1e-05)
    return (values * factor * norm_gain.astype(jnp.float32)).astype(jnp.bfloat16)


def gate_table(normed, router_weight, routes):
    logits = jnp.dot(normed, router_weight, preferred_element_type=jnp.float32)
    expert_ids = jnp.arange(router_weight.shape[1], dtype=jnp.int32)
    onehot = routes[:, :, None] == expert_ids[None, None, :]
    chosen = jnp.sum(jnp.where(onehot, logits[:, None, :], 0.0), axis=2)
    weights = jax.nn.softmax(chosen, axis=-1)
    return jnp.sum(jnp.where(onehot, weights[:, :, None], 0.0), axis=1)


def positions_of(segment_ids):
    index_row = jnp.arange(segment_ids.shape[0], dtype=jnp.int32)
    starts_here = jnp.concatenate([jnp.ones((1,), dtype=bool), segment_ids[1:] != segment_ids[:-1]])
    segment_start = lax.cummax(jnp.where(starts_here, index_row, 0), axis=0)
    return index_row - segment_start


def rotate(values, positions):
    half_width = values.shape[-1] // 2
    frequency = 10000.0 ** (-jnp.arange(half_width, dtype=jnp.float32) / half_width)
    angles = positions.astype(jnp.float32)[:, None] * frequency[None, :]
    angles = angles.reshape((values.shape[0],) + (1,) * (values.ndim - 2) + (half_width,))
    cosine = jnp.cos(angles)
    sine_part = jnp.sin(angles)
    leading = values[..., :half_width]
    trailing = values[..., half_width:]
    return jnp.concatenate(
        [leading * cosine - trailing * sine_part, trailing * cosine + leading * sine_part], axis=-1
    )


def project_kv(normed, weight, positions, first_block):
    projected = jnp.dot(normed, weight, preferred_element_type=jnp.float32)
    block_total = weight.shape[1] // HD
    blocks = projected.reshape(normed.shape[0], block_total, HD)
    block_index = first_block + jnp.arange(block_total, dtype=jnp.int32)
    turned = rotate(blocks, positions)
    chosen = jnp.where((block_index % 2 == 0)[None, :, None], turned, blocks)
    return chosen.astype(jnp.bfloat16).reshape(normed.shape[0], weight.shape[1])


def write_pages(kv_cache, page_table, rows):
    pages = jnp.arange(kv_cache.shape[0], dtype=jnp.int32)
    hit = page_table[None, :] == pages[:, None]
    placed = jnp.einsum(
        "pb,brc->prc", hit.astype(rows.dtype), rows, preferred_element_type=jnp.float32
    ).astype(kv_cache.dtype)
    return jnp.where(jnp.any(hit, axis=1)[:, None, None], placed, kv_cache)


def bit_orders(bits, parts):
    rest = list(range(1, bits))
    if not rest:
        return [[0]] * parts
    return [[0] + rest[j % len(rest):] + rest[:j % len(rest)] for j in range(parts)]


def reduce_to_owner(partial, axis):
    size = lax.axis_size(axis)
    bits = size.bit_length() - 1
    assert 1 << bits == size
    me = lax.axis_index(axis)
    rows, width = partial.shape
    block = rows // size
    parts = REDUCE_PARTS if width % REDUCE_PARTS == 0 else 1
    piece = width // parts
    outs = []
    for j, order in enumerate(bit_orders(bits, parts)):
        cols = partial[:, j * piece:(j + 1) * piece]
        cube = cols.reshape((2,) * bits + (block, piece))
        cube = jnp.transpose(cube, [bits - 1 - k for k in order] + [bits, bits + 1])
        current = cube.reshape(rows, piece)
        for k in order:
            half = current.shape[0] // 2
            mine = (me >> k) & 1
            keep = lax.dynamic_slice_in_dim(current, mine * half, half, 0)
            send = lax.dynamic_slice_in_dim(current, (1 - mine) * half, half, 0)
            got = lax.ppermute(send, axis, [(i, i ^ (1 << k)) for i in range(size)])
            current = (keep.astype(jnp.float32) + got.astype(jnp.float32)).astype(jnp.bfloat16)
        outs.append(current)
    return jnp.concatenate(outs, axis=1)


def attention_kernel(window, q_ref, cos_ref, sin_ref, k_ref, v_ref, qseg_ref, kseg_ref, gate_ref, out_ref):
    chunk = pl.program_id(0)
    blocks = pl.num_programs(0)
    start_block = jnp.clip(chunk - (window - 1), 0, blocks - window)
    start = pl.multiple_of(start_block * CHUNK, CHUNK)
    span = window * CHUNK
    keys = k_ref[:, pl.ds(start, span)]
    values = v_ref[pl.ds(start, span), :]
    key_seg = kseg_ref[:, pl.ds(start, span)]
    query_seg = qseg_ref[...]
    query_index = chunk * CHUNK + lax.broadcasted_iota(jnp.int32, (CHUNK, span), 0)
    key_index = start + lax.broadcasted_iota(jnp.int32, (CHUNK, span), 1)
    allowed = (query_seg == key_seg) & (key_index <= query_index)
    cosine = cos_ref[...]
    sine_part = sin_ref[...]
    scale_factor = HD ** (-0.5)
    experts = gate_ref.shape[1]
    for e in range(experts):
        raw = q_ref[:, e * HD:(e + 1) * HD]
        turned = raw * cosine + pltpu.roll(raw, HD // 2, 1) * sine_part
        queries = (turned * scale_factor).astype(jnp.bfloat16)
        scores = jnp.dot(queries, keys, preferred_element_type=jnp.float32)
        scores = jnp.where(allowed, scores, -1e30)
        top = jnp.max(scores, axis=1, keepdims=True)
        raised = jnp.exp(scores - top)
        inverse = 1.0 / jnp.sum(raised, axis=1, keepdims=True)
        probabilities = (raised * inverse).astype(jnp.bfloat16)
        attended = jnp.dot(probabilities, values, preferred_element_type=jnp.float32)
        out_ref[:, e * HD:(e + 1) * HD] = (attended * gate_ref[:, e:e + 1]).astype(out_ref.dtype)


def rope_tables(positions):
    half_width = HD // 2
    frequency = 10000.0 ** (-jnp.arange(half_width, dtype=jnp.float32) / half_width)
    angles = positions.astype(jnp.float32)[:, None] * frequency[None, :]
    cosine = jnp.cos(angles)
    sine_part = jnp.sin(angles)
    return (
        jnp.concatenate([cosine, cosine], axis=1),
        jnp.concatenate([-sine_part, sine_part], axis=1),
    )


def attend_window(raw_queries, positions, keys, values, segment_ids, gate_here):
    tokens, width = raw_queries.shape
    experts = width // HD
    blocks = tokens // CHUNK
    window = min(blocks, SEG_MOST // CHUNK + 1)
    cosine, sine_part = rope_tables(positions)
    seg_cols = segment_ids.reshape(tokens, 1)
    seg_row = segment_ids.reshape(1, tokens)
    return pl.pallas_call(
        lambda *refs: attention_kernel(window, *refs),
        grid=(blocks,),
        in_specs=[
            pl.BlockSpec((CHUNK, width), lambda i: (i, 0)),
            pl.BlockSpec((CHUNK, HD), lambda i: (i, 0)),
            pl.BlockSpec((CHUNK, HD), lambda i: (i, 0)),
            pl.BlockSpec((HD, tokens), lambda i: (0, 0)),
            pl.BlockSpec((tokens, HD), lambda i: (0, 0)),
            pl.BlockSpec((CHUNK, 1), lambda i: (i, 0)),
            pl.BlockSpec((1, tokens), lambda i: (0, 0)),
            pl.BlockSpec((CHUNK, experts), lambda i: (i, 0)),
        ],
        out_specs=pl.BlockSpec((CHUNK, width), lambda i: (i, 0)),
        out_shape=jax.ShapeDtypeStruct((tokens, width), jnp.bfloat16),
        cost_estimate=pl.CostEstimate(
            flops=4 * tokens * window * CHUNK * width,
            transcendentals=tokens * window * CHUNK * experts,
            bytes_accessed=tokens * width * 6 + 2 * tokens * HD * 2 + 2 * tokens * HD * 4,
        ),
    )(raw_queries, cosine, sine_part, jnp.transpose(keys), values, seg_cols, seg_row, gate_here)


def gather_from_all(block, axis):
    size = lax.axis_size(axis)
    bits = size.bit_length() - 1
    assert 1 << bits == size
    me = lax.axis_index(axis)
    rows, width = block.shape
    parts = REDUCE_PARTS if width % REDUCE_PARTS == 0 else 1
    piece = width // parts
    outs = []
    for j, forward in enumerate(bit_orders(bits, parts)):
        order = forward[::-1]
        current = block[:, j * piece:(j + 1) * piece]
        for k in order:
            got = lax.ppermute(current, axis, [(i, i ^ (1 << k)) for i in range(size)])
            upper = ((me >> k) & 1) == 1
            current = jnp.concatenate(
                [jnp.where(upper, got, current), jnp.where(upper, current, got)], axis=0
            )
        cube = current.reshape((2,) * bits + (rows, piece))
        old_axis = {order[bits - 1 - a]: a for a in range(bits)}
        cube = jnp.transpose(cube, [old_axis[bits - 1 - a] for a in range(bits)] + [bits, bits + 1])
        outs.append(cube.reshape(size * rows, piece))
    return jnp.concatenate(outs, axis=1)


def local(
    hidden,
    norm_gain,
    router_weight,
    kv_weight,
    query_weight,
    out_weight,
    routes,
    segment_ids,
    page_table,
    kv_cache,
):
    device_index = lax.axis_index("tensor")
    token_count = routes.shape[0]
    normed = gather_from_all(normalize(hidden, norm_gain), "tensor")
    gates = gate_table(normed, router_weight, routes)
    positions = positions_of(segment_ids)
    kv_width = kv_weight.shape[1]
    block_count = kv_width // HD
    own_rows = project_kv(normed, kv_weight, positions, device_index * block_count)
    new_cache = write_pages(kv_cache, page_table, own_rows.reshape(page_table.shape[0], PAGE, kv_width))
    partner_rows = swapped(own_rows, "tensor", 0)
    leading_first = device_index % 2 == 0
    key_rows = jnp.where(leading_first, own_rows, partner_rows)
    value_rows = jnp.where(leading_first, partner_rows, own_rows)
    pair_count = query_weight.shape[1] // HD
    raw_queries = jnp.dot(normed, query_weight, preferred_element_type=jnp.float32)
    first_expert = (device_index * pair_count) % EA
    gate_here = lax.dynamic_slice_in_dim(gates, first_expert, pair_count, 1)
    flat = attend_window(raw_queries, positions, key_rows, value_rows, segment_ids, gate_here)
    partial = jnp.dot(flat, out_weight, preferred_element_type=jnp.float32).astype(jnp.bfloat16)
    reduced = reduce_to_owner(partial, "tensor").astype(jnp.float32)
    attended_out = (hidden.astype(jnp.float32) + reduced).astype(jnp.bfloat16)
    return (attended_out, new_cache)


def solution(mesh):
    placed = (
        P(("dp", "tensor"), None),
        P(),
        P(),
        P(None, "tensor"),
        P(None, "tensor"),
        P("tensor", None),
        P("dp", None),
        P("dp"),
        P("dp"),
        P("dp", None, "tensor"),
    )
    return jax.shard_map(
        local,
        mesh=mesh,
        in_specs=placed,
        out_specs=(P(("dp", "tensor"), None), P("dp", None, "tensor")),
        check_vma=False,
    )
```

```python
import jax
import jax.numpy as jnp
from jax import lax
from jax.experimental import pallas as pl
from jax.experimental.pallas import tpu as pltpu
from jax.sharding import PartitionSpec as P

D = 2048
HD = 128
EA = 8
PAGE = 128
REDUCE_PARTS = 4
SEG_MOST = 512
CHUNK = 512


def swapped(array, axis, bit):
    return lax.ppermute(array, axis, [(i, i ^ 1 << bit) for i in range(lax.axis_size(axis))])


def normalize(hidden, norm_gain):
    values = hidden.astype(jnp.float32)
    factor = lax.rsqrt(jnp.mean(values * values, axis=-1, keepdims=True) + 1e-05)
    return (values * factor * norm_gain.astype(jnp.float32)).astype(jnp.bfloat16)


def gate_table(normed, router_weight, routes):
    logits = jnp.dot(normed, router_weight, preferred_element_type=jnp.float32)
    expert_ids = jnp.arange(router_weight.shape[1], dtype=jnp.int32)
    onehot = routes[:, :, None] == expert_ids[None, None, :]
    chosen = jnp.sum(jnp.where(onehot, logits[:, None, :], 0.0), axis=2)
    weights = jax.nn.softmax(chosen, axis=-1)
    return jnp.sum(jnp.where(onehot, weights[:, :, None], 0.0), axis=1)


def positions_of(segment_ids):
    index_row = jnp.arange(segment_ids.shape[0], dtype=jnp.int32)
    starts_here = jnp.concatenate([jnp.ones((1,), dtype=bool), segment_ids[1:] != segment_ids[:-1]])
    segment_start = lax.cummax(jnp.where(starts_here, index_row, 0), axis=0)
    return index_row - segment_start


def rotate(values, positions):
    half_width = values.shape[-1] // 2
    frequency = 10000.0 ** (-jnp.arange(half_width, dtype=jnp.float32) / half_width)
    angles = positions.astype(jnp.float32)[:, None] * frequency[None, :]
    angles = angles.reshape((values.shape[0],) + (1,) * (values.ndim - 2) + (half_width,))
    cosine = jnp.cos(angles)
    sine_part = jnp.sin(angles)
    leading = values[..., :half_width]
    trailing = values[..., half_width:]
    return jnp.concatenate(
        [leading * cosine - trailing * sine_part, trailing * cosine + leading * sine_part], axis=-1
    )


def project_kv(normed, weight, positions, first_block):
    projected = jnp.dot(normed, weight, preferred_element_type=jnp.float32)
    block_total = weight.shape[1] // HD
    blocks = projected.reshape(normed.shape[0], block_total, HD)
    block_index = first_block + jnp.arange(block_total, dtype=jnp.int32)
    turned = rotate(blocks, positions)
    chosen = jnp.where((block_index % 2 == 0)[None, :, None], turned, blocks)
    return chosen.astype(jnp.bfloat16).reshape(normed.shape[0], weight.shape[1])


def write_pages(kv_cache, page_table, rows):
    pages = jnp.arange(kv_cache.shape[0], dtype=jnp.int32)
    hit = page_table[None, :] == pages[:, None]
    placed = jnp.einsum(
        "pb,brc->prc", hit.astype(rows.dtype), rows, preferred_element_type=jnp.float32
    ).astype(kv_cache.dtype)
    return jnp.where(jnp.any(hit, axis=1)[:, None, None], placed, kv_cache)


def bit_orders(bits, parts):
    rest = list(range(1, bits))
    if not rest:
        return [[0]] * parts
    return [[0] + rest[j % len(rest):] + rest[:j % len(rest)] for j in range(parts)]


def reduce_to_owner(partial, axis):
    size = lax.axis_size(axis)
    bits = size.bit_length() - 1
    assert 1 << bits == size
    me = lax.axis_index(axis)
    rows, width = partial.shape
    block = rows // size
    parts = REDUCE_PARTS if width % REDUCE_PARTS == 0 else 1
    piece = width // parts
    outs = []
    for j, order in enumerate(bit_orders(bits, parts)):
        cols = partial[:, j * piece:(j + 1) * piece]
        cube = cols.reshape((2,) * bits + (block, piece))
        cube = jnp.transpose(cube, [bits - 1 - k for k in order] + [bits, bits + 1])
        current = cube.reshape(rows, piece)
        for k in order:
            half = current.shape[0] // 2
            mine = (me >> k) & 1
            keep = lax.dynamic_slice_in_dim(current, mine * half, half, 0)
            send = lax.dynamic_slice_in_dim(current, (1 - mine) * half, half, 0)
            got = lax.ppermute(send, axis, [(i, i ^ (1 << k)) for i in range(size)])
            current = (keep.astype(jnp.float32) + got.astype(jnp.float32)).astype(jnp.bfloat16)
        outs.append(current)
    return jnp.concatenate(outs, axis=1)


def attention_kernel(window, q_ref, cos_ref, sin_ref, k_ref, v_ref, qseg_ref, kseg_ref, gate_ref, out_ref):
    chunk = pl.program_id(0)
    blocks = pl.num_programs(0)
    start_block = jnp.clip(chunk - (window - 1), 0, blocks - window)
    start = pl.multiple_of(start_block * CHUNK, CHUNK)
    span = window * CHUNK
    keys = k_ref[:, pl.ds(start, span)]
    values = v_ref[pl.ds(start, span), :]
    key_seg = kseg_ref[:, pl.ds(start, span)]
    query_seg = qseg_ref[...]
    query_index = chunk * CHUNK + lax.broadcasted_iota(jnp.int32, (CHUNK, span), 0)
    key_index = start + lax.broadcasted_iota(jnp.int32, (CHUNK, span), 1)
    allowed = (query_seg == key_seg) & (key_index <= query_index)
    cosine = cos_ref[...]
    sine_part = sin_ref[...]
    scale_factor = HD ** (-0.5)
    experts = gate_ref.shape[1]
    for e in range(experts):
        raw = q_ref[:, e * HD:(e + 1) * HD]
        turned = raw * cosine + pltpu.roll(raw, HD // 2, 1) * sine_part
        queries = (turned * scale_factor).astype(jnp.bfloat16)
        scores = jnp.dot(queries, keys, preferred_element_type=jnp.float32)
        scores = jnp.where(allowed, scores, -1e30)
        top = jnp.max(scores, axis=1, keepdims=True)
        raised = jnp.exp(scores - top)
        inverse = 1.0 / jnp.sum(raised, axis=1, keepdims=True)
        probabilities = (raised * inverse).astype(jnp.bfloat16)
        attended = jnp.dot(probabilities, values, preferred_element_type=jnp.float32)
        out_ref[:, e * HD:(e + 1) * HD] = (attended * gate_ref[:, e:e + 1]).astype(out_ref.dtype)


def rope_tables(positions):
    half_width = HD // 2
    frequency = 10000.0 ** (-jnp.arange(half_width, dtype=jnp.float32) / half_width)
    angles = positions.astype(jnp.float32)[:, None] * frequency[None, :]
    cosine = jnp.cos(angles)
    sine_part = jnp.sin(angles)
    return (
        jnp.concatenate([cosine, cosine], axis=1),
        jnp.concatenate([-sine_part, sine_part], axis=1),
    )


def attend_window(raw_queries, positions, keys, values, segment_ids, gate_here):
    tokens, width = raw_queries.shape
    experts = width // HD
    blocks = tokens // CHUNK
    window = min(blocks, SEG_MOST // CHUNK + 1)
    cosine, sine_part = rope_tables(positions)
    seg_cols = segment_ids.reshape(tokens, 1)
    seg_row = segment_ids.reshape(1, tokens)
    return pl.pallas_call(
        lambda *refs: attention_kernel(window, *refs),
        grid=(blocks,),
        in_specs=[
            pl.BlockSpec((CHUNK, width), lambda i: (i, 0)),
            pl.BlockSpec((CHUNK, HD), lambda i: (i, 0)),
            pl.BlockSpec((CHUNK, HD), lambda i: (i, 0)),
            pl.BlockSpec((HD, tokens), lambda i: (0, 0)),
            pl.BlockSpec((tokens, HD), lambda i: (0, 0)),
            pl.BlockSpec((CHUNK, 1), lambda i: (i, 0)),
            pl.BlockSpec((1, tokens), lambda i: (0, 0)),
            pl.BlockSpec((CHUNK, experts), lambda i: (i, 0)),
        ],
        out_specs=pl.BlockSpec((CHUNK, width), lambda i: (i, 0)),
        out_shape=jax.ShapeDtypeStruct((tokens, width), jnp.bfloat16),
        cost_estimate=pl.CostEstimate(
            flops=4 * tokens * window * CHUNK * width,
            transcendentals=tokens * window * CHUNK * experts,
            bytes_accessed=tokens * width * 6 + 2 * tokens * HD * 2 + 2 * tokens * HD * 4,
        ),
    )(raw_queries, cosine, sine_part, jnp.transpose(keys), values, seg_cols, seg_row, gate_here)


def gather_from_all(block, axis):
    size = lax.axis_size(axis)
    bits = size.bit_length() - 1
    assert 1 << bits == size
    me = lax.axis_index(axis)
    rows, width = block.shape
    parts = REDUCE_PARTS if width % REDUCE_PARTS == 0 else 1
    piece = width // parts
    outs = []
    for j, forward in enumerate(bit_orders(bits, parts)):
        order = forward[::-1]
        current = block[:, j * piece:(j + 1) * piece]
        for k in order:
            got = lax.ppermute(current, axis, [(i, i ^ (1 << k)) for i in range(size)])
            upper = ((me >> k) & 1) == 1
            current = jnp.concatenate(
                [jnp.where(upper, got, current), jnp.where(upper, current, got)], axis=0
            )
        cube = current.reshape((2,) * bits + (rows, piece))
        old_axis = {order[bits - 1 - a]: a for a in range(bits)}
        cube = jnp.transpose(cube, [old_axis[bits - 1 - a] for a in range(bits)] + [bits, bits + 1])
        outs.append(cube.reshape(size * rows, piece))
    return jnp.concatenate(outs, axis=1)


def local(
    hidden,
    norm_gain,
    router_weight,
    kv_weight,
    query_weight,
    out_weight,
    routes,
    segment_ids,
    page_table,
    kv_cache,
):
    device_index = lax.axis_index("tensor")
    token_count = routes.shape[0]
    normed = gather_from_all(normalize(hidden, norm_gain), "tensor")
    gates = gate_table(normed, router_weight, routes)
    positions = positions_of(segment_ids)
    kv_width = kv_weight.shape[1]
    block_count = kv_width // HD
    own_rows = project_kv(normed, kv_weight, positions, device_index * block_count)
    new_cache = write_pages(kv_cache, page_table, own_rows.reshape(page_table.shape[0], PAGE, kv_width))
    partner_rows = swapped(own_rows, "tensor", 0)
    leading_first = device_index % 2 == 0
    key_rows = jnp.where(leading_first, own_rows, partner_rows)
    value_rows = jnp.where(leading_first, partner_rows, own_rows)
    pair_count = query_weight.shape[1] // HD
    raw_queries = jnp.dot(normed, query_weight, preferred_element_type=jnp.float32)
    first_expert = (device_index * pair_count) % EA
    gate_here = lax.dynamic_slice_in_dim(gates, first_expert, pair_count, 1)
    flat = attend_window(raw_queries, positions, key_rows, value_rows, segment_ids, gate_here)
    partial = jnp.dot(flat, out_weight, preferred_element_type=jnp.float32).astype(jnp.bfloat16)
    reduced = reduce_to_owner(partial, "tensor").astype(jnp.float32)
    attended_out = (hidden.astype(jnp.float32) + reduced).astype(jnp.bfloat16)
    return (attended_out, new_cache)


def solution(mesh):
    placed = (
        P(("dp", "tensor"), None),
        P(),
        P(),
        P(None, "tensor"),
        P(None, "tensor"),
        P("tensor", None),
        P("dp", None),
        P("dp"),
        P("dp"),
        P("dp", None, "tensor"),
    )
    return jax.shard_map(
        local,
        mesh=mesh,
        in_specs=placed,
        out_specs=(P(("dp", "tensor"), None), P("dp", None, "tensor")),
        check_vma=False,
    )
```

```python
import jax
import jax.numpy as jnp
from jax import lax
from jax.experimental import pallas as pl
from jax.experimental.pallas import tpu as pltpu
from jax.sharding import PartitionSpec as P

D = 2048
HD = 128
EA = 8
PAGE = 128
REDUCE_PARTS = 4
SEG_MOST = 512
CHUNK = 256


def swapped(array, axis, bit):
    return lax.ppermute(array, axis, [(i, i ^ 1 << bit) for i in range(lax.axis_size(axis))])


def normalize(hidden, norm_gain):
    values = hidden.astype(jnp.float32)
    factor = lax.rsqrt(jnp.mean(values * values, axis=-1, keepdims=True) + 1e-05)
    return (values * factor * norm_gain.astype(jnp.float32)).astype(jnp.bfloat16)


def gate_table(normed, router_weight, routes):
    logits = jnp.dot(normed, router_weight, preferred_element_type=jnp.float32)
    expert_ids = jnp.arange(router_weight.shape[1], dtype=jnp.int32)
    onehot = routes[:, :, None] == expert_ids[None, None, :]
    chosen = jnp.sum(jnp.where(onehot, logits[:, None, :], 0.0), axis=2)
    weights = jax.nn.softmax(chosen, axis=-1)
    return jnp.sum(jnp.where(onehot, weights[:, :, None], 0.0), axis=1)


def positions_of(segment_ids):
    index_row = jnp.arange(segment_ids.shape[0], dtype=jnp.int32)
    starts_here = jnp.concatenate([jnp.ones((1,), dtype=bool), segment_ids[1:] != segment_ids[:-1]])
    segment_start = lax.cummax(jnp.where(starts_here, index_row, 0), axis=0)
    return index_row - segment_start


def rotate(values, positions):
    half_width = values.shape[-1] // 2
    frequency = 10000.0 ** (-jnp.arange(half_width, dtype=jnp.float32) / half_width)
    angles = positions.astype(jnp.float32)[:, None] * frequency[None, :]
    angles = angles.reshape((values.shape[0],) + (1,) * (values.ndim - 2) + (half_width,))
    cosine = jnp.cos(angles)
    sine_part = jnp.sin(angles)
    leading = values[..., :half_width]
    trailing = values[..., half_width:]
    return jnp.concatenate(
        [leading * cosine - trailing * sine_part, trailing * cosine + leading * sine_part], axis=-1
    )


def project_kv(normed, weight, positions, first_block):
    projected = jnp.dot(normed, weight, preferred_element_type=jnp.float32)
    block_total = weight.shape[1] // HD
    blocks = projected.reshape(normed.shape[0], block_total, HD)
    block_index = first_block + jnp.arange(block_total, dtype=jnp.int32)
    turned = rotate(blocks, positions)
    chosen = jnp.where((block_index % 2 == 0)[None, :, None], turned, blocks)
    return chosen.astype(jnp.bfloat16).reshape(normed.shape[0], weight.shape[1])


def write_pages(kv_cache, page_table, rows):
    pages = jnp.arange(kv_cache.shape[0], dtype=jnp.int32)
    hit = page_table[None, :] == pages[:, None]
    placed = jnp.einsum(
        "pb,brc->prc", hit.astype(rows.dtype), rows, preferred_element_type=jnp.float32
    ).astype(kv_cache.dtype)
    return jnp.where(jnp.any(hit, axis=1)[:, None, None], placed, kv_cache)


def bit_orders(bits, parts):
    rest = list(range(1, bits))
    if not rest:
        return [[0]] * parts
    return [[0] + rest[j % len(rest):] + rest[:j % len(rest)] for j in range(parts)]


def reduce_to_owner(partial, axis):
    size = lax.axis_size(axis)
    bits = size.bit_length() - 1
    assert 1 << bits == size
    me = lax.axis_index(axis)
    rows, width = partial.shape
    block = rows // size
    parts = REDUCE_PARTS if width % REDUCE_PARTS == 0 else 1
    piece = width // parts
    outs = []
    for j, order in enumerate(bit_orders(bits, parts)):
        cols = partial[:, j * piece:(j + 1) * piece]
        cube = cols.reshape((2,) * bits + (block, piece))
        cube = jnp.transpose(cube, [bits - 1 - k for k in order] + [bits, bits + 1])
        current = cube.reshape(rows, piece)
        for k in order:
            half = current.shape[0] // 2
            mine = (me >> k) & 1
            keep = lax.dynamic_slice_in_dim(current, mine * half, half, 0)
            send = lax.dynamic_slice_in_dim(current, (1 - mine) * half, half, 0)
            got = lax.ppermute(send, axis, [(i, i ^ (1 << k)) for i in range(size)])
            current = (keep.astype(jnp.float32) + got.astype(jnp.float32)).astype(jnp.bfloat16)
        outs.append(current)
    return jnp.concatenate(outs, axis=1)


def attention_kernel(
    window, x_ref, wq_ref, wo_ref, cos_ref, sin_ref, k_ref, v_ref, qseg_ref, kseg_ref, gate_ref, out_ref, gated_ref
):
    chunk = pl.program_id(0)
    blocks = pl.num_programs(0)
    start_block = jnp.clip(chunk - (window - 1), 0, blocks - window)
    start = pl.multiple_of(start_block * CHUNK, CHUNK)
    span = window * CHUNK
    keys = k_ref[:, pl.ds(start, span)]
    values = v_ref[pl.ds(start, span), :]
    key_seg = kseg_ref[:, pl.ds(start, span)]
    query_seg = qseg_ref[...]
    query_index = chunk * CHUNK + lax.broadcasted_iota(jnp.int32, (CHUNK, span), 0)
    key_index = start + lax.broadcasted_iota(jnp.int32, (CHUNK, span), 1)
    allowed = (query_seg == key_seg) & (key_index <= query_index)
    cosine = cos_ref[...]
    sine_part = sin_ref[...]
    scale_factor = HD ** (-0.5)
    raw_all = jnp.dot(x_ref[...], wq_ref[...], preferred_element_type=jnp.float32)
    experts = gate_ref.shape[1]
    for e in range(experts):
        raw = raw_all[:, e * HD:(e + 1) * HD]
        turned = raw * cosine + pltpu.roll(raw, HD // 2, 1) * sine_part
        queries = (turned * scale_factor).astype(jnp.bfloat16)
        scores = jnp.dot(queries, keys, preferred_element_type=jnp.float32)
        scores = jnp.where(allowed, scores, -1e30)
        top = jnp.max(scores, axis=1, keepdims=True)
        raised = jnp.exp(scores - top)
        inverse = 1.0 / jnp.sum(raised, axis=1, keepdims=True)
        probabilities = (raised * inverse).astype(jnp.bfloat16)
        attended = jnp.dot(probabilities, values, preferred_element_type=jnp.float32)
        gated_ref[:, e * HD:(e + 1) * HD] = (attended * gate_ref[:, e:e + 1]).astype(jnp.bfloat16)
    out_ref[...] = jnp.dot(gated_ref[...], wo_ref[...], preferred_element_type=jnp.float32).astype(
        out_ref.dtype
    )


def rope_tables(positions):
    half_width = HD // 2
    frequency = 10000.0 ** (-jnp.arange(half_width, dtype=jnp.float32) / half_width)
    angles = positions.astype(jnp.float32)[:, None] * frequency[None, :]
    cosine = jnp.cos(angles)
    sine_part = jnp.sin(angles)
    return (
        jnp.concatenate([cosine, cosine], axis=1),
        jnp.concatenate([-sine_part, sine_part], axis=1),
    )


def attend_window(normed, query_weight, out_weight, positions, keys, values, segment_ids, gate_here):
    tokens, width = normed.shape
    pair_width = query_weight.shape[1]
    experts = pair_width // HD
    blocks = tokens // CHUNK
    window = min(blocks, SEG_MOST // CHUNK + 1)
    cosine, sine_part = rope_tables(positions)
    seg_cols = segment_ids.reshape(tokens, 1)
    seg_row = segment_ids.reshape(1, tokens)
    return pl.pallas_call(
        lambda *refs: attention_kernel(window, *refs),
        grid=(blocks,),
        in_specs=[
            pl.BlockSpec((CHUNK, width), lambda i: (i, 0)),
            pl.BlockSpec((width, pair_width), lambda i: (0, 0)),
            pl.BlockSpec((pair_width, width), lambda i: (0, 0)),
            pl.BlockSpec((CHUNK, HD), lambda i: (i, 0)),
            pl.BlockSpec((CHUNK, HD), lambda i: (i, 0)),
            pl.BlockSpec((HD, tokens), lambda i: (0, 0)),
            pl.BlockSpec((tokens, HD), lambda i: (0, 0)),
            pl.BlockSpec((CHUNK, 1), lambda i: (i, 0)),
            pl.BlockSpec((1, tokens), lambda i: (0, 0)),
            pl.BlockSpec((CHUNK, experts), lambda i: (i, 0)),
        ],
        out_specs=pl.BlockSpec((CHUNK, width), lambda i: (i, 0)),
        out_shape=jax.ShapeDtypeStruct((tokens, width), jnp.bfloat16),
        scratch_shapes=[pltpu.VMEM((CHUNK, pair_width), jnp.bfloat16)],
        cost_estimate=pl.CostEstimate(
            flops=4 * tokens * window * CHUNK * pair_width + 4 * tokens * width * pair_width,
            transcendentals=tokens * window * CHUNK * experts,
            bytes_accessed=2 * tokens * width * 2 + 2 * width * pair_width * 2 + 2 * tokens * HD * 4,
        ),
    )(normed, query_weight, out_weight, cosine, sine_part, jnp.transpose(keys), values, seg_cols, seg_row, gate_here)


def gather_from_all(block, axis):
    size = lax.axis_size(axis)
    bits = size.bit_length() - 1
    assert 1 << bits == size
    me = lax.axis_index(axis)
    rows, width = block.shape
    parts = REDUCE_PARTS if width % REDUCE_PARTS == 0 else 1
    piece = width // parts
    outs = []
    for j, forward in enumerate(bit_orders(bits, parts)):
        order = forward[::-1]
        current = block[:, j * piece:(j + 1) * piece]
        for k in order:
            got = lax.ppermute(current, axis, [(i, i ^ (1 << k)) for i in range(size)])
            upper = ((me >> k) & 1) == 1
            current = jnp.concatenate(
                [jnp.where(upper, got, current), jnp.where(upper, current, got)], axis=0
            )
        cube = current.reshape((2,) * bits + (rows, piece))
        old_axis = {order[bits - 1 - a]: a for a in range(bits)}
        cube = jnp.transpose(cube, [old_axis[bits - 1 - a] for a in range(bits)] + [bits, bits + 1])
        outs.append(cube.reshape(size * rows, piece))
    return jnp.concatenate(outs, axis=1)


def local(
    hidden,
    norm_gain,
    router_weight,
    kv_weight,
    query_weight,
    out_weight,
    routes,
    segment_ids,
    page_table,
    kv_cache,
):
    device_index = lax.axis_index("tensor")
    token_count = routes.shape[0]
    normed = gather_from_all(normalize(hidden, norm_gain), "tensor")
    gates = gate_table(normed, router_weight, routes)
    positions = positions_of(segment_ids)
    kv_width = kv_weight.shape[1]
    block_count = kv_width // HD
    own_rows = project_kv(normed, kv_weight, positions, device_index * block_count)
    new_cache = write_pages(kv_cache, page_table, own_rows.reshape(page_table.shape[0], PAGE, kv_width))
    partner_rows = swapped(own_rows, "tensor", 0)
    leading_first = device_index % 2 == 0
    key_rows = jnp.where(leading_first, own_rows, partner_rows)
    value_rows = jnp.where(leading_first, partner_rows, own_rows)
    pair_count = query_weight.shape[1] // HD
    first_expert = (device_index * pair_count) % EA
    gate_here = lax.dynamic_slice_in_dim(gates, first_expert, pair_count, 1)
    partial = attend_window(
        normed, query_weight, out_weight, positions, key_rows, value_rows, segment_ids, gate_here
    )
    reduced = reduce_to_owner(partial, "tensor").astype(jnp.float32)
    attended_out = (hidden.astype(jnp.float32) + reduced).astype(jnp.bfloat16)
    return (attended_out, new_cache)


def solution(mesh):
    placed = (
        P(("dp", "tensor"), None),
        P(),
        P(),
        P(None, "tensor"),
        P(None, "tensor"),
        P("tensor", None),
        P("dp", None),
        P("dp"),
        P("dp"),
        P("dp", None, "tensor"),
    )
    return jax.shard_map(
        local,
        mesh=mesh,
        in_specs=placed,
        out_specs=(P(("dp", "tensor"), None), P("dp", None, "tensor")),
        check_vma=False,
    )
```

```python
import jax
import jax.numpy as jnp
from jax import lax
from jax.experimental import pallas as pl
from jax.experimental.pallas import tpu as pltpu
from jax.sharding import PartitionSpec as P

D = 2048
HD = 128
EA = 8
PAGE = 128
REDUCE_PARTS = 2
SEG_MOST = 512
CHUNK = 256


def swapped(array, axis, bit):
    return lax.ppermute(array, axis, [(i, i ^ 1 << bit) for i in range(lax.axis_size(axis))])


def normalize(hidden, norm_gain):
    values = hidden.astype(jnp.float32)
    factor = lax.rsqrt(jnp.mean(values * values, axis=-1, keepdims=True) + 1e-05)
    return (values * factor * norm_gain.astype(jnp.float32)).astype(jnp.bfloat16)


def gate_table(normed, router_weight, routes):
    logits = jnp.dot(normed, router_weight, preferred_element_type=jnp.float32)
    expert_ids = jnp.arange(router_weight.shape[1], dtype=jnp.int32)
    onehot = routes[:, :, None] == expert_ids[None, None, :]
    chosen = jnp.sum(jnp.where(onehot, logits[:, None, :], 0.0), axis=2)
    weights = jax.nn.softmax(chosen, axis=-1)
    return jnp.sum(jnp.where(onehot, weights[:, :, None], 0.0), axis=1)


def positions_of(segment_ids):
    index_row = jnp.arange(segment_ids.shape[0], dtype=jnp.int32)
    starts_here = jnp.concatenate([jnp.ones((1,), dtype=bool), segment_ids[1:] != segment_ids[:-1]])
    segment_start = lax.cummax(jnp.where(starts_here, index_row, 0), axis=0)
    return index_row - segment_start


def rotate(values, positions):
    half_width = values.shape[-1] // 2
    frequency = 10000.0 ** (-jnp.arange(half_width, dtype=jnp.float32) / half_width)
    angles = positions.astype(jnp.float32)[:, None] * frequency[None, :]
    angles = angles.reshape((values.shape[0],) + (1,) * (values.ndim - 2) + (half_width,))
    cosine = jnp.cos(angles)
    sine_part = jnp.sin(angles)
    leading = values[..., :half_width]
    trailing = values[..., half_width:]
    return jnp.concatenate(
        [leading * cosine - trailing * sine_part, trailing * cosine + leading * sine_part], axis=-1
    )


def project_kv(normed, weight, positions, first_block):
    projected = jnp.dot(normed, weight, preferred_element_type=jnp.float32)
    block_total = weight.shape[1] // HD
    blocks = projected.reshape(normed.shape[0], block_total, HD)
    block_index = first_block + jnp.arange(block_total, dtype=jnp.int32)
    turned = rotate(blocks, positions)
    chosen = jnp.where((block_index % 2 == 0)[None, :, None], turned, blocks)
    return chosen.astype(jnp.bfloat16).reshape(normed.shape[0], weight.shape[1])


def write_pages(kv_cache, page_table, rows):
    pages = jnp.arange(kv_cache.shape[0], dtype=jnp.int32)
    hit = page_table[None, :] == pages[:, None]
    placed = jnp.einsum(
        "pb,brc->prc", hit.astype(rows.dtype), rows, preferred_element_type=jnp.float32
    ).astype(kv_cache.dtype)
    return jnp.where(jnp.any(hit, axis=1)[:, None, None], placed, kv_cache)


def bit_orders(bits, parts):
    rest = list(range(1, bits))
    if not rest:
        return [[0]] * parts
    stride = max(1, len(rest) // parts)
    return [[0] + rest[j * stride % len(rest):] + rest[:j * stride % len(rest)] for j in range(parts)]


def reduce_to_owner(partial, axis):
    size = lax.axis_size(axis)
    bits = size.bit_length() - 1
    assert 1 << bits == size
    me = lax.axis_index(axis)
    rows, width = partial.shape
    block = rows // size
    parts = REDUCE_PARTS if width % REDUCE_PARTS == 0 else 1
    piece = width // parts
    outs = []
    for j, order in enumerate(bit_orders(bits, parts)):
        cols = partial[:, j * piece:(j + 1) * piece]
        cube = cols.reshape((2,) * bits + (block, piece))
        cube = jnp.transpose(cube, [bits - 1 - k for k in order] + [bits, bits + 1])
        current = cube.reshape(rows, piece)
        for k in order:
            half = current.shape[0] // 2
            mine = (me >> k) & 1
            keep = lax.dynamic_slice_in_dim(current, mine * half, half, 0)
            send = lax.dynamic_slice_in_dim(current, (1 - mine) * half, half, 0)
            got = lax.ppermute(send, axis, [(i, i ^ (1 << k)) for i in range(size)])
            current = (keep.astype(jnp.float32) + got.astype(jnp.float32)).astype(jnp.bfloat16)
        outs.append(current)
    return jnp.concatenate(outs, axis=1)


def attention_kernel(window, q_ref, cos_ref, sin_ref, k_ref, v_ref, qseg_ref, kseg_ref, gate_ref, out_ref):
    chunk = pl.program_id(0)
    blocks = pl.num_programs(0)
    start_block = jnp.clip(chunk - (window - 1), 0, blocks - window)
    start = pl.multiple_of(start_block * CHUNK, CHUNK)
    span = window * CHUNK
    keys = k_ref[:, pl.ds(start, span)]
    values = v_ref[pl.ds(start, span), :]
    key_seg = kseg_ref[:, pl.ds(start, span)]
    query_seg = qseg_ref[...]
    query_index = chunk * CHUNK + lax.broadcasted_iota(jnp.int32, (CHUNK, span), 0)
    key_index = start + lax.broadcasted_iota(jnp.int32, (CHUNK, span), 1)
    allowed = (query_seg == key_seg) & (key_index <= query_index)
    cosine = cos_ref[...]
    sine_part = sin_ref[...]
    scale_factor = HD ** (-0.5)
    experts = gate_ref.shape[1]
    for e in range(experts):
        raw = q_ref[:, e * HD:(e + 1) * HD]
        turned = raw * cosine + pltpu.roll(raw, HD // 2, 1) * sine_part
        queries = (turned * scale_factor).astype(jnp.bfloat16)
        scores = jnp.dot(queries, keys, preferred_element_type=jnp.float32)
        scores = jnp.where(allowed, scores, -1e30)
        top = jnp.max(scores, axis=1, keepdims=True)
        raised = jnp.exp(scores - top)
        inverse = 1.0 / jnp.sum(raised, axis=1, keepdims=True)
        probabilities = (raised * inverse).astype(jnp.bfloat16)
        attended = jnp.dot(probabilities, values, preferred_element_type=jnp.float32)
        out_ref[:, e * HD:(e + 1) * HD] = (attended * gate_ref[:, e:e + 1]).astype(out_ref.dtype)


def rope_tables(positions):
    half_width = HD // 2
    frequency = 10000.0 ** (-jnp.arange(half_width, dtype=jnp.float32) / half_width)
    angles = positions.astype(jnp.float32)[:, None] * frequency[None, :]
    cosine = jnp.cos(angles)
    sine_part = jnp.sin(angles)
    return (
        jnp.concatenate([cosine, cosine], axis=1),
        jnp.concatenate([-sine_part, sine_part], axis=1),
    )


def attend_window(raw_queries, positions, keys, values, segment_ids, gate_here):
    tokens, width = raw_queries.shape
    experts = width // HD
    blocks = tokens // CHUNK
    window = min(blocks, SEG_MOST // CHUNK + 1)
    cosine, sine_part = rope_tables(positions)
    seg_cols = segment_ids.reshape(tokens, 1)
    seg_row = segment_ids.reshape(1, tokens)
    return pl.pallas_call(
        lambda *refs: attention_kernel(window, *refs),
        grid=(blocks,),
        in_specs=[
            pl.BlockSpec((CHUNK, width), lambda i: (i, 0)),
            pl.BlockSpec((CHUNK, HD), lambda i: (i, 0)),
            pl.BlockSpec((CHUNK, HD), lambda i: (i, 0)),
            pl.BlockSpec((HD, tokens), lambda i: (0, 0)),
            pl.BlockSpec((tokens, HD), lambda i: (0, 0)),
            pl.BlockSpec((CHUNK, 1), lambda i: (i, 0)),
            pl.BlockSpec((1, tokens), lambda i: (0, 0)),
            pl.BlockSpec((CHUNK, experts), lambda i: (i, 0)),
        ],
        out_specs=pl.BlockSpec((CHUNK, width), lambda i: (i, 0)),
        out_shape=jax.ShapeDtypeStruct((tokens, width), jnp.bfloat16),
        cost_estimate=pl.CostEstimate(
            flops=4 * tokens * window * CHUNK * width,
            transcendentals=tokens * window * CHUNK * experts,
            bytes_accessed=tokens * width * 6 + 2 * tokens * HD * 2 + 2 * tokens * HD * 4,
        ),
    )(raw_queries, cosine, sine_part, jnp.transpose(keys), values, seg_cols, seg_row, gate_here)


def gather_from_all(block, axis):
    size = lax.axis_size(axis)
    bits = size.bit_length() - 1
    assert 1 << bits == size
    me = lax.axis_index(axis)
    rows, width = block.shape
    parts = REDUCE_PARTS if width % REDUCE_PARTS == 0 else 1
    piece = width // parts
    outs = []
    for j, forward in enumerate(bit_orders(bits, parts)):
        order = forward[::-1]
        current = block[:, j * piece:(j + 1) * piece]
        for k in order:
            got = lax.ppermute(current, axis, [(i, i ^ (1 << k)) for i in range(size)])
            upper = ((me >> k) & 1) == 1
            current = jnp.concatenate(
                [jnp.where(upper, got, current), jnp.where(upper, current, got)], axis=0
            )
        cube = current.reshape((2,) * bits + (rows, piece))
        old_axis = {order[bits - 1 - a]: a for a in range(bits)}
        cube = jnp.transpose(cube, [old_axis[bits - 1 - a] for a in range(bits)] + [bits, bits + 1])
        outs.append(cube.reshape(size * rows, piece))
    return jnp.concatenate(outs, axis=1)


def local(
    hidden,
    norm_gain,
    router_weight,
    kv_weight,
    query_weight,
    out_weight,
    routes,
    segment_ids,
    page_table,
    kv_cache,
):
    device_index = lax.axis_index("tensor")
    token_count = routes.shape[0]
    normed = gather_from_all(normalize(hidden, norm_gain), "tensor")
    gates = gate_table(normed, router_weight, routes)
    positions = positions_of(segment_ids)
    kv_width = kv_weight.shape[1]
    block_count = kv_width // HD
    own_rows = project_kv(normed, kv_weight, positions, device_index * block_count)
    new_cache = write_pages(kv_cache, page_table, own_rows.reshape(page_table.shape[0], PAGE, kv_width))
    partner_rows = swapped(own_rows, "tensor", 0)
    leading_first = device_index % 2 == 0
    key_rows = jnp.where(leading_first, own_rows, partner_rows)
    value_rows = jnp.where(leading_first, partner_rows, own_rows)
    pair_count = query_weight.shape[1] // HD
    raw_queries = jnp.dot(normed, query_weight, preferred_element_type=jnp.float32)
    first_expert = (device_index * pair_count) % EA
    gate_here = lax.dynamic_slice_in_dim(gates, first_expert, pair_count, 1)
    flat = attend_window(raw_queries, positions, key_rows, value_rows, segment_ids, gate_here)
    partial = jnp.dot(flat, out_weight, preferred_element_type=jnp.float32).astype(jnp.bfloat16)
    reduced = reduce_to_owner(partial, "tensor").astype(jnp.float32)
    attended_out = (hidden.astype(jnp.float32) + reduced).astype(jnp.bfloat16)
    return (attended_out, new_cache)


def solution(mesh):
    placed = (
        P(("dp", "tensor"), None),
        P(),
        P(),
        P(None, "tensor"),
        P(None, "tensor"),
        P("tensor", None),
        P("dp", None),
        P("dp"),
        P("dp"),
        P("dp", None, "tensor"),
    )
    return jax.shard_map(
        local,
        mesh=mesh,
        in_specs=placed,
        out_specs=(P(("dp", "tensor"), None), P("dp", None, "tensor")),
        check_vma=False,
    )
```

```python
import jax
import jax.numpy as jnp
from jax import lax
from jax.experimental import pallas as pl
from jax.experimental.pallas import tpu as pltpu
from jax.sharding import PartitionSpec as P

D = 2048
HD = 128
EA = 8
PAGE = 128
REDUCE_PARTS = 4
SEG_MOST = 512
CHUNK = 256


def swapped(array, axis, bit):
    return lax.ppermute(array, axis, [(i, i ^ 1 << bit) for i in range(lax.axis_size(axis))])


def normalize(hidden, norm_gain):
    values = hidden.astype(jnp.float32)
    factor = lax.rsqrt(jnp.mean(values * values, axis=-1, keepdims=True) + 1e-05)
    return (values * factor * norm_gain.astype(jnp.float32)).astype(jnp.bfloat16)


def gate_table(normed, router_weight, routes):
    logits = jnp.dot(normed, router_weight, preferred_element_type=jnp.float32)
    expert_ids = jnp.arange(router_weight.shape[1], dtype=jnp.int32)
    onehot = routes[:, :, None] == expert_ids[None, None, :]
    chosen = jnp.sum(jnp.where(onehot, logits[:, None, :], 0.0), axis=2)
    weights = jax.nn.softmax(chosen, axis=-1)
    return jnp.sum(jnp.where(onehot, weights[:, :, None], 0.0), axis=1)


def positions_of(segment_ids):
    index_row = jnp.arange(segment_ids.shape[0], dtype=jnp.int32)
    starts_here = jnp.concatenate([jnp.ones((1,), dtype=bool), segment_ids[1:] != segment_ids[:-1]])
    segment_start = lax.cummax(jnp.where(starts_here, index_row, 0), axis=0)
    return index_row - segment_start


def rotate(values, positions):
    half_width = values.shape[-1] // 2
    frequency = 10000.0 ** (-jnp.arange(half_width, dtype=jnp.float32) / half_width)
    angles = positions.astype(jnp.float32)[:, None] * frequency[None, :]
    angles = angles.reshape((values.shape[0],) + (1,) * (values.ndim - 2) + (half_width,))
    cosine = jnp.cos(angles)
    sine_part = jnp.sin(angles)
    leading = values[..., :half_width]
    trailing = values[..., half_width:]
    return jnp.concatenate(
        [leading * cosine - trailing * sine_part, trailing * cosine + leading * sine_part], axis=-1
    )


def project_kv(normed, weight, tables, first_block):
    cosine, sine_part = tables
    projected = jnp.dot(normed, weight, preferred_element_type=jnp.float32)
    block_total = weight.shape[1] // HD
    blocks = projected.reshape(normed.shape[0], block_total, HD)
    block_index = first_block + jnp.arange(block_total, dtype=jnp.int32)
    turned = blocks * cosine[:, None, :] + jnp.roll(blocks, HD // 2, axis=2) * sine_part[:, None, :]
    chosen = jnp.where((block_index % 2 == 0)[None, :, None], turned, blocks)
    return chosen.astype(jnp.bfloat16).reshape(normed.shape[0], weight.shape[1])


def write_pages(kv_cache, page_table, rows):
    pages = jnp.arange(kv_cache.shape[0], dtype=jnp.int32)
    hit = page_table[None, :] == pages[:, None]
    placed = jnp.einsum(
        "pb,brc->prc", hit.astype(rows.dtype), rows, preferred_element_type=jnp.float32
    ).astype(kv_cache.dtype)
    return jnp.where(jnp.any(hit, axis=1)[:, None, None], placed, kv_cache)


def bit_orders(bits, parts):
    rest = list(range(1, bits))
    if not rest:
        return [[0]] * parts
    return [[0] + rest[j % len(rest):] + rest[:j % len(rest)] for j in range(parts)]


def reduce_to_owner(partial, axis):
    size = lax.axis_size(axis)
    bits = size.bit_length() - 1
    assert 1 << bits == size
    me = lax.axis_index(axis)
    rows, width = partial.shape
    block = rows // size
    parts = REDUCE_PARTS if width % REDUCE_PARTS == 0 else 1
    piece = width // parts
    outs = []
    for j, order in enumerate(bit_orders(bits, parts)):
        cols = partial[:, j * piece:(j + 1) * piece]
        cube = cols.reshape((2,) * bits + (block, piece))
        cube = jnp.transpose(cube, [bits - 1 - k for k in order] + [bits, bits + 1])
        current = cube.reshape(rows, piece)
        for k in order:
            half = current.shape[0] // 2
            mine = (me >> k) & 1
            keep = lax.dynamic_slice_in_dim(current, mine * half, half, 0)
            send = lax.dynamic_slice_in_dim(current, (1 - mine) * half, half, 0)
            got = lax.ppermute(send, axis, [(i, i ^ (1 << k)) for i in range(size)])
            current = (keep.astype(jnp.float32) + got.astype(jnp.float32)).astype(jnp.bfloat16)
        outs.append(current)
    return jnp.concatenate(outs, axis=1)


def attention_kernel(window, q_ref, cos_ref, sin_ref, k_ref, v_ref, qseg_ref, kseg_ref, gate_ref, out_ref):
    chunk = pl.program_id(0)
    blocks = pl.num_programs(0)
    start_block = jnp.clip(chunk - (window - 1), 0, blocks - window)
    start = pl.multiple_of(start_block * CHUNK, CHUNK)
    span = window * CHUNK
    keys = k_ref[:, pl.ds(start, span)]
    values = v_ref[pl.ds(start, span), :]
    key_seg = kseg_ref[:, pl.ds(start, span)]
    query_seg = qseg_ref[...]
    query_index = chunk * CHUNK + lax.broadcasted_iota(jnp.int32, (CHUNK, span), 0)
    key_index = start + lax.broadcasted_iota(jnp.int32, (CHUNK, span), 1)
    allowed = (query_seg == key_seg) & (key_index <= query_index)
    cosine = cos_ref[...]
    sine_part = sin_ref[...]
    scale_factor = HD ** (-0.5)
    experts = gate_ref.shape[1]
    for e in range(experts):
        raw = q_ref[:, e * HD:(e + 1) * HD]
        turned = raw * cosine + pltpu.roll(raw, HD // 2, 1) * sine_part
        queries = (turned * scale_factor).astype(jnp.bfloat16)
        scores = jnp.dot(queries, keys, preferred_element_type=jnp.float32)
        scores = jnp.where(allowed, scores, -1e30)
        top = jnp.max(scores, axis=1, keepdims=True)
        raised = jnp.exp(scores - top)
        inverse = 1.0 / jnp.sum(raised, axis=1, keepdims=True)
        probabilities = (raised * inverse).astype(jnp.bfloat16)
        attended = jnp.dot(probabilities, values, preferred_element_type=jnp.float32)
        out_ref[:, e * HD:(e + 1) * HD] = (attended * gate_ref[:, e:e + 1]).astype(out_ref.dtype)


def rope_tables(positions):
    half_width = HD // 2
    frequency = 10000.0 ** (-jnp.arange(half_width, dtype=jnp.float32) / half_width)
    angles = positions.astype(jnp.float32)[:, None] * frequency[None, :]
    cosine = jnp.cos(angles)
    sine_part = jnp.sin(angles)
    return (
        jnp.concatenate([cosine, cosine], axis=1),
        jnp.concatenate([-sine_part, sine_part], axis=1),
    )


def attend_window(raw_queries, tables, keys, values, segment_ids, gate_here):
    tokens, width = raw_queries.shape
    experts = width // HD
    blocks = tokens // CHUNK
    window = min(blocks, SEG_MOST // CHUNK + 1)
    cosine, sine_part = tables
    seg_cols = segment_ids.reshape(tokens, 1)
    seg_row = segment_ids.reshape(1, tokens)
    return pl.pallas_call(
        lambda *refs: attention_kernel(window, *refs),
        grid=(blocks,),
        in_specs=[
            pl.BlockSpec((CHUNK, width), lambda i: (i, 0)),
            pl.BlockSpec((CHUNK, HD), lambda i: (i, 0)),
            pl.BlockSpec((CHUNK, HD), lambda i: (i, 0)),
            pl.BlockSpec((HD, tokens), lambda i: (0, 0)),
            pl.BlockSpec((tokens, HD), lambda i: (0, 0)),
            pl.BlockSpec((CHUNK, 1), lambda i: (i, 0)),
            pl.BlockSpec((1, tokens), lambda i: (0, 0)),
            pl.BlockSpec((CHUNK, experts), lambda i: (i, 0)),
        ],
        out_specs=pl.BlockSpec((CHUNK, width), lambda i: (i, 0)),
        out_shape=jax.ShapeDtypeStruct((tokens, width), jnp.bfloat16),
        cost_estimate=pl.CostEstimate(
            flops=4 * tokens * window * CHUNK * width,
            transcendentals=tokens * window * CHUNK * experts,
            bytes_accessed=tokens * width * 6 + 2 * tokens * HD * 2 + 2 * tokens * HD * 4,
        ),
    )(raw_queries, cosine, sine_part, jnp.transpose(keys), values, seg_cols, seg_row, gate_here)


def gather_from_all(block, axis):
    size = lax.axis_size(axis)
    bits = size.bit_length() - 1
    assert 1 << bits == size
    me = lax.axis_index(axis)
    rows, width = block.shape
    parts = REDUCE_PARTS if width % REDUCE_PARTS == 0 else 1
    piece = width // parts
    outs = []
    for j, forward in enumerate(bit_orders(bits, parts)):
        order = forward[::-1]
        current = block[:, j * piece:(j + 1) * piece]
        for k in order:
            got = lax.ppermute(current, axis, [(i, i ^ (1 << k)) for i in range(size)])
            upper = ((me >> k) & 1) == 1
            current = jnp.concatenate(
                [jnp.where(upper, got, current), jnp.where(upper, current, got)], axis=0
            )
        cube = current.reshape((2,) * bits + (rows, piece))
        old_axis = {order[bits - 1 - a]: a for a in range(bits)}
        cube = jnp.transpose(cube, [old_axis[bits - 1 - a] for a in range(bits)] + [bits, bits + 1])
        outs.append(cube.reshape(size * rows, piece))
    return jnp.concatenate(outs, axis=1)


def local(
    hidden,
    norm_gain,
    router_weight,
    kv_weight,
    query_weight,
    out_weight,
    routes,
    segment_ids,
    page_table,
    kv_cache,
):
    device_index = lax.axis_index("tensor")
    token_count = routes.shape[0]
    normed = gather_from_all(normalize(hidden, norm_gain), "tensor")
    gates = gate_table(normed, router_weight, routes)
    positions = positions_of(segment_ids)
    kv_width = kv_weight.shape[1]
    block_count = kv_width // HD
    tables = rope_tables(positions)
    own_rows = project_kv(normed, kv_weight, tables, device_index * block_count)
    new_cache = write_pages(kv_cache, page_table, own_rows.reshape(page_table.shape[0], PAGE, kv_width))
    partner_rows = swapped(own_rows, "tensor", 0)
    leading_first = device_index % 2 == 0
    key_rows = jnp.where(leading_first, own_rows, partner_rows)
    value_rows = jnp.where(leading_first, partner_rows, own_rows)
    pair_count = query_weight.shape[1] // HD
    raw_queries = jnp.dot(normed, query_weight, preferred_element_type=jnp.float32)
    first_expert = (device_index * pair_count) % EA
    gate_here = lax.dynamic_slice_in_dim(gates, first_expert, pair_count, 1)
    flat = attend_window(raw_queries, tables, key_rows, value_rows, segment_ids, gate_here)
    partial = jnp.dot(flat, out_weight, preferred_element_type=jnp.float32).astype(jnp.bfloat16)
    reduced = reduce_to_owner(partial, "tensor").astype(jnp.float32)
    attended_out = (hidden.astype(jnp.float32) + reduced).astype(jnp.bfloat16)
    return (attended_out, new_cache)


def solution(mesh):
    placed = (
        P(("dp", "tensor"), None),
        P(),
        P(),
        P(None, "tensor"),
        P(None, "tensor"),
        P("tensor", None),
        P("dp", None),
        P("dp"),
        P("dp"),
        P("dp", None, "tensor"),
    )
    return jax.shard_map(
        local,
        mesh=mesh,
        in_specs=placed,
        out_specs=(P(("dp", "tensor"), None), P("dp", None, "tensor")),
        check_vma=False,
    )
```

```python
import jax
import jax.numpy as jnp
from jax import lax
from jax.experimental import pallas as pl
from jax.experimental.pallas import tpu as pltpu
from jax.sharding import PartitionSpec as P

D = 2048
HD = 128
EA = 8
PAGE = 128
REDUCE_PARTS = 4
SEG_MOST = 512
CHUNK = 256


def swapped(array, axis, bit):
    return lax.ppermute(array, axis, [(i, i ^ 1 << bit) for i in range(lax.axis_size(axis))])


def normalize(hidden, norm_gain):
    values = hidden.astype(jnp.float32)
    factor = lax.rsqrt(jnp.mean(values * values, axis=-1, keepdims=True) + 1e-05)
    return (values * factor * norm_gain.astype(jnp.float32)).astype(jnp.bfloat16)


def gate_table(normed, router_weight, routes):
    logits = jnp.dot(normed, router_weight, preferred_element_type=jnp.float32)
    expert_ids = jnp.arange(router_weight.shape[1], dtype=jnp.int32)
    onehot = routes[:, :, None] == expert_ids[None, None, :]
    chosen = jnp.sum(jnp.where(onehot, logits[:, None, :], 0.0), axis=2)
    weights = jax.nn.softmax(chosen, axis=-1)
    return jnp.sum(jnp.where(onehot, weights[:, :, None], 0.0), axis=1)


def positions_of(segment_ids):
    index_row = jnp.arange(segment_ids.shape[0], dtype=jnp.int32)
    starts_here = jnp.concatenate([jnp.ones((1,), dtype=bool), segment_ids[1:] != segment_ids[:-1]])
    segment_start = lax.cummax(jnp.where(starts_here, index_row, 0), axis=0)
    return index_row - segment_start


def rotate(values, positions):
    half_width = values.shape[-1] // 2
    frequency = 10000.0 ** (-jnp.arange(half_width, dtype=jnp.float32) / half_width)
    angles = positions.astype(jnp.float32)[:, None] * frequency[None, :]
    angles = angles.reshape((values.shape[0],) + (1,) * (values.ndim - 2) + (half_width,))
    cosine = jnp.cos(angles)
    sine_part = jnp.sin(angles)
    leading = values[..., :half_width]
    trailing = values[..., half_width:]
    return jnp.concatenate(
        [leading * cosine - trailing * sine_part, trailing * cosine + leading * sine_part], axis=-1
    )


def project_kv(normed, weight, positions, first_block):
    projected = jnp.dot(normed, weight, preferred_element_type=jnp.float32)
    block_total = weight.shape[1] // HD
    blocks = projected.reshape(normed.shape[0], block_total, HD)
    block_index = first_block + jnp.arange(block_total, dtype=jnp.int32)
    turned = rotate(blocks, positions)
    chosen = jnp.where((block_index % 2 == 0)[None, :, None], turned, blocks)
    return chosen.astype(jnp.bfloat16).reshape(normed.shape[0], weight.shape[1])


def write_pages(kv_cache, page_table, rows):
    pages = jnp.arange(kv_cache.shape[0], dtype=jnp.int32)
    hit = page_table[None, :] == pages[:, None]
    placed = jnp.einsum(
        "pb,brc->prc", hit.astype(rows.dtype), rows, preferred_element_type=jnp.float32
    ).astype(kv_cache.dtype)
    return jnp.where(jnp.any(hit, axis=1)[:, None, None], placed, kv_cache)


def bit_orders(bits, parts):
    rest = list(range(1, bits))
    if not rest:
        return [[0]] * parts
    return [[0] + rest[j % len(rest):] + rest[:j % len(rest)] for j in range(parts)]


def reduce_to_owner(flat, out_weight, axis):
    size = lax.axis_size(axis)
    bits = size.bit_length() - 1
    assert 1 << bits == size
    me = lax.axis_index(axis)
    rows = flat.shape[0]
    width = out_weight.shape[1]
    block = rows // size
    parts = REDUCE_PARTS if width % REDUCE_PARTS == 0 else 1
    piece = width // parts
    outs = []
    for j, order in enumerate(bit_orders(bits, parts)):
        cols = jnp.dot(
            flat, out_weight[:, j * piece:(j + 1) * piece], preferred_element_type=jnp.float32
        ).astype(jnp.bfloat16)
        cube = cols.reshape((2,) * bits + (block, piece))
        cube = jnp.transpose(cube, [bits - 1 - k for k in order] + [bits, bits + 1])
        current = cube.reshape(rows, piece)
        for k in order:
            half = current.shape[0] // 2
            mine = (me >> k) & 1
            keep = lax.dynamic_slice_in_dim(current, mine * half, half, 0)
            send = lax.dynamic_slice_in_dim(current, (1 - mine) * half, half, 0)
            got = lax.ppermute(send, axis, [(i, i ^ (1 << k)) for i in range(size)])
            current = (keep.astype(jnp.float32) + got.astype(jnp.float32)).astype(jnp.bfloat16)
        outs.append(current)
    return jnp.concatenate(outs, axis=1)


def attention_kernel(window, q_ref, cos_ref, sin_ref, k_ref, v_ref, qseg_ref, kseg_ref, gate_ref, out_ref):
    chunk = pl.program_id(0)
    blocks = pl.num_programs(0)
    start_block = jnp.clip(chunk - (window - 1), 0, blocks - window)
    start = pl.multiple_of(start_block * CHUNK, CHUNK)
    span = window * CHUNK
    keys = k_ref[:, pl.ds(start, span)]
    values = v_ref[pl.ds(start, span), :]
    key_seg = kseg_ref[:, pl.ds(start, span)]
    query_seg = qseg_ref[...]
    query_index = chunk * CHUNK + lax.broadcasted_iota(jnp.int32, (CHUNK, span), 0)
    key_index = start + lax.broadcasted_iota(jnp.int32, (CHUNK, span), 1)
    allowed = (query_seg == key_seg) & (key_index <= query_index)
    cosine = cos_ref[...]
    sine_part = sin_ref[...]
    scale_factor = HD ** (-0.5)
    experts = gate_ref.shape[1]
    for e in range(experts):
        raw = q_ref[:, e * HD:(e + 1) * HD]
        turned = raw * cosine + pltpu.roll(raw, HD // 2, 1) * sine_part
        queries = (turned * scale_factor).astype(jnp.bfloat16)
        scores = jnp.dot(queries, keys, preferred_element_type=jnp.float32)
        scores = jnp.where(allowed, scores, -1e30)
        top = jnp.max(scores, axis=1, keepdims=True)
        raised = jnp.exp(scores - top)
        inverse = 1.0 / jnp.sum(raised, axis=1, keepdims=True)
        probabilities = (raised * inverse).astype(jnp.bfloat16)
        attended = jnp.dot(probabilities, values, preferred_element_type=jnp.float32)
        out_ref[:, e * HD:(e + 1) * HD] = (attended * gate_ref[:, e:e + 1]).astype(out_ref.dtype)


def rope_tables(positions):
    half_width = HD // 2
    frequency = 10000.0 ** (-jnp.arange(half_width, dtype=jnp.float32) / half_width)
    angles = positions.astype(jnp.float32)[:, None] * frequency[None, :]
    cosine = jnp.cos(angles)
    sine_part = jnp.sin(angles)
    return (
        jnp.concatenate([cosine, cosine], axis=1),
        jnp.concatenate([-sine_part, sine_part], axis=1),
    )


def attend_window(raw_queries, positions, keys, values, segment_ids, gate_here):
    tokens, width = raw_queries.shape
    experts = width // HD
    blocks = tokens // CHUNK
    window = min(blocks, SEG_MOST // CHUNK + 1)
    cosine, sine_part = rope_tables(positions)
    seg_cols = segment_ids.reshape(tokens, 1)
    seg_row = segment_ids.reshape(1, tokens)
    return pl.pallas_call(
        lambda *refs: attention_kernel(window, *refs),
        grid=(blocks,),
        in_specs=[
            pl.BlockSpec((CHUNK, width), lambda i: (i, 0)),
            pl.BlockSpec((CHUNK, HD), lambda i: (i, 0)),
            pl.BlockSpec((CHUNK, HD), lambda i: (i, 0)),
            pl.BlockSpec((HD, tokens), lambda i: (0, 0)),
            pl.BlockSpec((tokens, HD), lambda i: (0, 0)),
            pl.BlockSpec((CHUNK, 1), lambda i: (i, 0)),
            pl.BlockSpec((1, tokens), lambda i: (0, 0)),
            pl.BlockSpec((CHUNK, experts), lambda i: (i, 0)),
        ],
        out_specs=pl.BlockSpec((CHUNK, width), lambda i: (i, 0)),
        out_shape=jax.ShapeDtypeStruct((tokens, width), jnp.bfloat16),
        cost_estimate=pl.CostEstimate(
            flops=4 * tokens * window * CHUNK * width,
            transcendentals=tokens * window * CHUNK * experts,
            bytes_accessed=tokens * width * 6 + 2 * tokens * HD * 2 + 2 * tokens * HD * 4,
        ),
    )(raw_queries, cosine, sine_part, jnp.transpose(keys), values, seg_cols, seg_row, gate_here)


def gather_from_all(block, axis):
    size = lax.axis_size(axis)
    bits = size.bit_length() - 1
    assert 1 << bits == size
    me = lax.axis_index(axis)
    rows, width = block.shape
    parts = REDUCE_PARTS if width % REDUCE_PARTS == 0 else 1
    piece = width // parts
    outs = []
    for j, forward in enumerate(bit_orders(bits, parts)):
        order = forward[::-1]
        current = block[:, j * piece:(j + 1) * piece]
        for k in order:
            got = lax.ppermute(current, axis, [(i, i ^ (1 << k)) for i in range(size)])
            upper = ((me >> k) & 1) == 1
            current = jnp.concatenate(
                [jnp.where(upper, got, current), jnp.where(upper, current, got)], axis=0
            )
        cube = current.reshape((2,) * bits + (rows, piece))
        old_axis = {order[bits - 1 - a]: a for a in range(bits)}
        cube = jnp.transpose(cube, [old_axis[bits - 1 - a] for a in range(bits)] + [bits, bits + 1])
        outs.append(cube.reshape(size * rows, piece))
    return jnp.concatenate(outs, axis=1)


def local(
    hidden,
    norm_gain,
    router_weight,
    kv_weight,
    query_weight,
    out_weight,
    routes,
    segment_ids,
    page_table,
    kv_cache,
):
    device_index = lax.axis_index("tensor")
    token_count = routes.shape[0]
    normed = gather_from_all(normalize(hidden, norm_gain), "tensor")
    gates = gate_table(normed, router_weight, routes)
    positions = positions_of(segment_ids)
    kv_width = kv_weight.shape[1]
    block_count = kv_width // HD
    own_rows = project_kv(normed, kv_weight, positions, device_index * block_count)
    new_cache = write_pages(kv_cache, page_table, own_rows.reshape(page_table.shape[0], PAGE, kv_width))
    partner_rows = swapped(own_rows, "tensor", 0)
    leading_first = device_index % 2 == 0
    key_rows = jnp.where(leading_first, own_rows, partner_rows)
    value_rows = jnp.where(leading_first, partner_rows, own_rows)
    pair_count = query_weight.shape[1] // HD
    raw_queries = jnp.dot(normed, query_weight, preferred_element_type=jnp.float32)
    first_expert = (device_index * pair_count) % EA
    gate_here = lax.dynamic_slice_in_dim(gates, first_expert, pair_count, 1)
    flat = attend_window(raw_queries, positions, key_rows, value_rows, segment_ids, gate_here)
    reduced = reduce_to_owner(flat, out_weight, "tensor").astype(jnp.float32)
    attended_out = (hidden.astype(jnp.float32) + reduced).astype(jnp.bfloat16)
    return (attended_out, new_cache)


def solution(mesh):
    placed = (
        P(("dp", "tensor"), None),
        P(),
        P(),
        P(None, "tensor"),
        P(None, "tensor"),
        P("tensor", None),
        P("dp", None),
        P("dp"),
        P("dp"),
        P("dp", None, "tensor"),
    )
    return jax.shard_map(
        local,
        mesh=mesh,
        in_specs=placed,
        out_specs=(P(("dp", "tensor"), None), P("dp", None, "tensor")),
        check_vma=False,
    )
```

```python
import jax
import jax.numpy as jnp
from jax import lax
from jax.experimental import pallas as pl
from jax.experimental.pallas import tpu as pltpu
from jax.sharding import PartitionSpec as P

D = 2048
HD = 128
EA = 8
PAGE = 128
REDUCE_PARTS = 4
SEG_MOST = 512
CHUNK = 256


def swapped(array, axis, bit):
    return lax.ppermute(array, axis, [(i, i ^ 1 << bit) for i in range(lax.axis_size(axis))])


def normalize(hidden, norm_gain):
    values = hidden.astype(jnp.float32)
    factor = lax.rsqrt(jnp.mean(values * values, axis=-1, keepdims=True) + 1e-05)
    return (values * factor * norm_gain.astype(jnp.float32)).astype(jnp.bfloat16)


def split_dot(pieces, weight):
    total = None
    start = 0
    for piece in pieces:
        width = piece.shape[1]
        term = jnp.dot(piece, weight[start:start + width], preferred_element_type=jnp.float32)
        total = term if total is None else total + term
        start += width
    return total


def gate_table(logits, routes):
    expert_ids = jnp.arange(logits.shape[1], dtype=jnp.int32)
    onehot = routes[:, :, None] == expert_ids[None, None, :]
    chosen = jnp.sum(jnp.where(onehot, logits[:, None, :], 0.0), axis=2)
    weights = jax.nn.softmax(chosen, axis=-1)
    return jnp.sum(jnp.where(onehot, weights[:, :, None], 0.0), axis=1)


def positions_of(segment_ids):
    index_row = jnp.arange(segment_ids.shape[0], dtype=jnp.int32)
    starts_here = jnp.concatenate([jnp.ones((1,), dtype=bool), segment_ids[1:] != segment_ids[:-1]])
    segment_start = lax.cummax(jnp.where(starts_here, index_row, 0), axis=0)
    return index_row - segment_start


def rotate(values, positions):
    half_width = values.shape[-1] // 2
    frequency = 10000.0 ** (-jnp.arange(half_width, dtype=jnp.float32) / half_width)
    angles = positions.astype(jnp.float32)[:, None] * frequency[None, :]
    angles = angles.reshape((values.shape[0],) + (1,) * (values.ndim - 2) + (half_width,))
    cosine = jnp.cos(angles)
    sine_part = jnp.sin(angles)
    leading = values[..., :half_width]
    trailing = values[..., half_width:]
    return jnp.concatenate(
        [leading * cosine - trailing * sine_part, trailing * cosine + leading * sine_part], axis=-1
    )


def project_kv(pieces, weight, positions, first_block):
    projected = split_dot(pieces, weight)
    tokens = projected.shape[0]
    block_total = weight.shape[1] // HD
    blocks = projected.reshape(tokens, block_total, HD)
    block_index = first_block + jnp.arange(block_total, dtype=jnp.int32)
    turned = rotate(blocks, positions)
    chosen = jnp.where((block_index % 2 == 0)[None, :, None], turned, blocks)
    return chosen.astype(jnp.bfloat16).reshape(tokens, weight.shape[1])


def write_pages(kv_cache, page_table, rows):
    pages = jnp.arange(kv_cache.shape[0], dtype=jnp.int32)
    hit = page_table[None, :] == pages[:, None]
    placed = jnp.einsum(
        "pb,brc->prc", hit.astype(rows.dtype), rows, preferred_element_type=jnp.float32
    ).astype(kv_cache.dtype)
    return jnp.where(jnp.any(hit, axis=1)[:, None, None], placed, kv_cache)


def bit_orders(bits, parts):
    rest = list(range(1, bits))
    if not rest:
        return [[0]] * parts
    return [[0] + rest[j % len(rest):] + rest[:j % len(rest)] for j in range(parts)]


def reduce_to_owner(partial, axis):
    size = lax.axis_size(axis)
    bits = size.bit_length() - 1
    assert 1 << bits == size
    me = lax.axis_index(axis)
    rows, width = partial.shape
    block = rows // size
    parts = REDUCE_PARTS if width % REDUCE_PARTS == 0 else 1
    piece = width // parts
    outs = []
    for j, order in enumerate(bit_orders(bits, parts)):
        cols = partial[:, j * piece:(j + 1) * piece]
        cube = cols.reshape((2,) * bits + (block, piece))
        cube = jnp.transpose(cube, [bits - 1 - k for k in order] + [bits, bits + 1])
        current = cube.reshape(rows, piece)
        for k in order:
            half = current.shape[0] // 2
            mine = (me >> k) & 1
            keep = lax.dynamic_slice_in_dim(current, mine * half, half, 0)
            send = lax.dynamic_slice_in_dim(current, (1 - mine) * half, half, 0)
            got = lax.ppermute(send, axis, [(i, i ^ (1 << k)) for i in range(size)])
            current = (keep.astype(jnp.float32) + got.astype(jnp.float32)).astype(jnp.bfloat16)
        outs.append(current)
    return jnp.concatenate(outs, axis=1)


def attention_kernel(window, q_ref, cos_ref, sin_ref, k_ref, v_ref, qseg_ref, kseg_ref, gate_ref, out_ref):
    chunk = pl.program_id(0)
    blocks = pl.num_programs(0)
    start_block = jnp.clip(chunk - (window - 1), 0, blocks - window)
    start = pl.multiple_of(start_block * CHUNK, CHUNK)
    span = window * CHUNK
    keys = k_ref[:, pl.ds(start, span)]
    values = v_ref[pl.ds(start, span), :]
    key_seg = kseg_ref[:, pl.ds(start, span)]
    query_seg = qseg_ref[...]
    query_index = chunk * CHUNK + lax.broadcasted_iota(jnp.int32, (CHUNK, span), 0)
    key_index = start + lax.broadcasted_iota(jnp.int32, (CHUNK, span), 1)
    allowed = (query_seg == key_seg) & (key_index <= query_index)
    cosine = cos_ref[...]
    sine_part = sin_ref[...]
    scale_factor = HD ** (-0.5)
    experts = gate_ref.shape[1]
    for e in range(experts):
        raw = q_ref[:, e * HD:(e + 1) * HD]
        turned = raw * cosine + pltpu.roll(raw, HD // 2, 1) * sine_part
        queries = (turned * scale_factor).astype(jnp.bfloat16)
        scores = jnp.dot(queries, keys, preferred_element_type=jnp.float32)
        scores = jnp.where(allowed, scores, -1e30)
        top = jnp.max(scores, axis=1, keepdims=True)
        raised = jnp.exp(scores - top)
        inverse = 1.0 / jnp.sum(raised, axis=1, keepdims=True)
        probabilities = (raised * inverse).astype(jnp.bfloat16)
        attended = jnp.dot(probabilities, values, preferred_element_type=jnp.float32)
        out_ref[:, e * HD:(e + 1) * HD] = (attended * gate_ref[:, e:e + 1]).astype(out_ref.dtype)


def rope_tables(positions):
    half_width = HD // 2
    frequency = 10000.0 ** (-jnp.arange(half_width, dtype=jnp.float32) / half_width)
    angles = positions.astype(jnp.float32)[:, None] * frequency[None, :]
    cosine = jnp.cos(angles)
    sine_part = jnp.sin(angles)
    return (
        jnp.concatenate([cosine, cosine], axis=1),
        jnp.concatenate([-sine_part, sine_part], axis=1),
    )


def attend_window(raw_queries, positions, keys, values, segment_ids, gate_here):
    tokens, width = raw_queries.shape
    experts = width // HD
    blocks = tokens // CHUNK
    window = min(blocks, SEG_MOST // CHUNK + 1)
    cosine, sine_part = rope_tables(positions)
    seg_cols = segment_ids.reshape(tokens, 1)
    seg_row = segment_ids.reshape(1, tokens)
    return pl.pallas_call(
        lambda *refs: attention_kernel(window, *refs),
        grid=(blocks,),
        in_specs=[
            pl.BlockSpec((CHUNK, width), lambda i: (i, 0)),
            pl.BlockSpec((CHUNK, HD), lambda i: (i, 0)),
            pl.BlockSpec((CHUNK, HD), lambda i: (i, 0)),
            pl.BlockSpec((HD, tokens), lambda i: (0, 0)),
            pl.BlockSpec((tokens, HD), lambda i: (0, 0)),
            pl.BlockSpec((CHUNK, 1), lambda i: (i, 0)),
            pl.BlockSpec((1, tokens), lambda i: (0, 0)),
            pl.BlockSpec((CHUNK, experts), lambda i: (i, 0)),
        ],
        out_specs=pl.BlockSpec((CHUNK, width), lambda i: (i, 0)),
        out_shape=jax.ShapeDtypeStruct((tokens, width), jnp.bfloat16),
        cost_estimate=pl.CostEstimate(
            flops=4 * tokens * window * CHUNK * width,
            transcendentals=tokens * window * CHUNK * experts,
            bytes_accessed=tokens * width * 6 + 2 * tokens * HD * 2 + 2 * tokens * HD * 4,
        ),
    )(raw_queries, cosine, sine_part, jnp.transpose(keys), values, seg_cols, seg_row, gate_here)


def gather_from_all(block, axis):
    size = lax.axis_size(axis)
    bits = size.bit_length() - 1
    assert 1 << bits == size
    me = lax.axis_index(axis)
    rows, width = block.shape
    parts = REDUCE_PARTS if width % REDUCE_PARTS == 0 else 1
    piece = width // parts
    outs = []
    for j, forward in enumerate(bit_orders(bits, parts)):
        order = forward[::-1]
        current = block[:, j * piece:(j + 1) * piece]
        for k in order:
            got = lax.ppermute(current, axis, [(i, i ^ (1 << k)) for i in range(size)])
            upper = ((me >> k) & 1) == 1
            current = jnp.concatenate(
                [jnp.where(upper, got, current), jnp.where(upper, current, got)], axis=0
            )
        cube = current.reshape((2,) * bits + (rows, piece))
        old_axis = {order[bits - 1 - a]: a for a in range(bits)}
        cube = jnp.transpose(cube, [old_axis[bits - 1 - a] for a in range(bits)] + [bits, bits + 1])
        outs.append(cube.reshape(size * rows, piece))
    return outs


def local(
    hidden,
    norm_gain,
    router_weight,
    kv_weight,
    query_weight,
    out_weight,
    routes,
    segment_ids,
    page_table,
    kv_cache,
):
    device_index = lax.axis_index("tensor")
    token_count = routes.shape[0]
    pieces = gather_from_all(normalize(hidden, norm_gain), "tensor")
    gates = gate_table(split_dot(pieces, router_weight), routes)
    positions = positions_of(segment_ids)
    kv_width = kv_weight.shape[1]
    block_count = kv_width // HD
    own_rows = project_kv(pieces, kv_weight, positions, device_index * block_count)
    new_cache = write_pages(kv_cache, page_table, own_rows.reshape(page_table.shape[0], PAGE, kv_width))
    partner_rows = swapped(own_rows, "tensor", 0)
    leading_first = device_index % 2 == 0
    key_rows = jnp.where(leading_first, own_rows, partner_rows)
    value_rows = jnp.where(leading_first, partner_rows, own_rows)
    pair_count = query_weight.shape[1] // HD
    raw_queries = split_dot(pieces, query_weight)
    first_expert = (device_index * pair_count) % EA
    gate_here = lax.dynamic_slice_in_dim(gates, first_expert, pair_count, 1)
    flat = attend_window(raw_queries, positions, key_rows, value_rows, segment_ids, gate_here)
    partial = jnp.dot(flat, out_weight, preferred_element_type=jnp.float32).astype(jnp.bfloat16)
    reduced = reduce_to_owner(partial, "tensor").astype(jnp.float32)
    attended_out = (hidden.astype(jnp.float32) + reduced).astype(jnp.bfloat16)
    return (attended_out, new_cache)


def solution(mesh):
    placed = (
        P(("dp", "tensor"), None),
        P(),
        P(),
        P(None, "tensor"),
        P(None, "tensor"),
        P("tensor", None),
        P("dp", None),
        P("dp"),
        P("dp"),
        P("dp", None, "tensor"),
    )
    return jax.shard_map(
        local,
        mesh=mesh,
        in_specs=placed,
        out_specs=(P(("dp", "tensor"), None), P("dp", None, "tensor")),
        check_vma=False,
    )
```

```python
import jax
import jax.numpy as jnp
from jax import lax
from jax.experimental import pallas as pl
from jax.experimental.pallas import tpu as pltpu
from jax.sharding import PartitionSpec as P

D = 2048
HD = 128
EA = 8
PAGE = 128
REDUCE_PARTS = 4
SEG_MOST = 512
CHUNK = 256


def swapped(array, axis, bit):
    return lax.ppermute(array, axis, [(i, i ^ 1 << bit) for i in range(lax.axis_size(axis))])


def normalize(hidden, norm_gain):
    values = hidden.astype(jnp.float32)
    factor = lax.rsqrt(jnp.mean(values * values, axis=-1, keepdims=True) + 1e-05)
    return (values * factor * norm_gain.astype(jnp.float32)).astype(jnp.bfloat16)


def gate_table(normed, router_weight, routes):
    logits = jnp.dot(normed, router_weight, preferred_element_type=jnp.float32)
    expert_ids = jnp.arange(router_weight.shape[1], dtype=jnp.int32)
    onehot = routes[:, :, None] == expert_ids[None, None, :]
    chosen = jnp.sum(jnp.where(onehot, logits[:, None, :], 0.0), axis=2)
    weights = jax.nn.softmax(chosen, axis=-1)
    return jnp.sum(jnp.where(onehot, weights[:, :, None], 0.0), axis=1)


def positions_of(segment_ids):
    index_row = jnp.arange(segment_ids.shape[0], dtype=jnp.int32)
    starts_here = jnp.concatenate([jnp.ones((1,), dtype=bool), segment_ids[1:] != segment_ids[:-1]])
    segment_start = lax.cummax(jnp.where(starts_here, index_row, 0), axis=0)
    return index_row - segment_start


def rotate(values, positions):
    half_width = values.shape[-1] // 2
    frequency = 10000.0 ** (-jnp.arange(half_width, dtype=jnp.float32) / half_width)
    angles = positions.astype(jnp.float32)[:, None] * frequency[None, :]
    angles = angles.reshape((values.shape[0],) + (1,) * (values.ndim - 2) + (half_width,))
    cosine = jnp.cos(angles)
    sine_part = jnp.sin(angles)
    leading = values[..., :half_width]
    trailing = values[..., half_width:]
    return jnp.concatenate(
        [leading * cosine - trailing * sine_part, trailing * cosine + leading * sine_part], axis=-1
    )


def project_kv(normed, weight, positions, first_block):
    projected = jnp.dot(normed, weight, preferred_element_type=jnp.float32)
    block_total = weight.shape[1] // HD
    blocks = projected.reshape(normed.shape[0], block_total, HD)
    block_index = first_block + jnp.arange(block_total, dtype=jnp.int32)
    turned = rotate(blocks, positions)
    chosen = jnp.where((block_index % 2 == 0)[None, :, None], turned, blocks)
    return chosen.astype(jnp.bfloat16).reshape(normed.shape[0], weight.shape[1])


def write_pages(kv_cache, page_table, rows):
    pages = jnp.arange(kv_cache.shape[0], dtype=jnp.int32)
    hit = page_table[None, :] == pages[:, None]
    placed = jnp.einsum(
        "pb,brc->prc", hit.astype(rows.dtype), rows, preferred_element_type=jnp.float32
    ).astype(kv_cache.dtype)
    return jnp.where(jnp.any(hit, axis=1)[:, None, None], placed, kv_cache)


def bit_orders(bits, parts):
    rest = list(range(1, bits))
    if not rest:
        return [[0]] * parts
    return [[0] + rest[j % len(rest):] + rest[:j % len(rest)] for j in range(parts)]


def reduce_to_owner(partial, axis):
    size = lax.axis_size(axis)
    bits = size.bit_length() - 1
    assert 1 << bits == size
    me = lax.axis_index(axis)
    rows, width = partial.shape
    block = rows // size
    parts = REDUCE_PARTS if width % REDUCE_PARTS == 0 else 1
    piece = width // parts
    outs = []
    for j, order in enumerate(bit_orders(bits, parts)):
        cols = partial[:, j * piece:(j + 1) * piece]
        cube = cols.reshape((2,) * bits + (block, piece))
        cube = jnp.transpose(cube, [bits - 1 - k for k in order] + [bits, bits + 1])
        current = cube.reshape(rows, piece)
        for k in order:
            half = current.shape[0] // 2
            mine = (me >> k) & 1
            keep = lax.dynamic_slice_in_dim(current, mine * half, half, 0)
            send = lax.dynamic_slice_in_dim(current, (1 - mine) * half, half, 0)
            got = lax.ppermute(send, axis, [(i, i ^ (1 << k)) for i in range(size)])
            current = (keep.astype(jnp.float32) + got.astype(jnp.float32)).astype(jnp.bfloat16)
        outs.append(current)
    return jnp.concatenate(outs, axis=1)


def attention_kernel(window, q_ref, cos_ref, sin_ref, k_ref, v_ref, qseg_ref, kseg_ref, gate_ref, out_ref):
    chunk = pl.program_id(0)
    blocks = pl.num_programs(0)
    start_block = jnp.clip(chunk - (window - 1), 0, blocks - window)
    start = pl.multiple_of(start_block * CHUNK, CHUNK)
    span = window * CHUNK
    keys = k_ref[:, pl.ds(start, span)]
    values = v_ref[pl.ds(start, span), :]
    key_seg = kseg_ref[:, pl.ds(start, span)]
    query_seg = qseg_ref[...]
    query_index = chunk * CHUNK + lax.broadcasted_iota(jnp.int32, (CHUNK, span), 0)
    key_index = start + lax.broadcasted_iota(jnp.int32, (CHUNK, span), 1)
    allowed = (query_seg == key_seg) & (key_index <= query_index)
    cosine = cos_ref[...]
    sine_part = sin_ref[...]
    scale_factor = HD ** (-0.5)
    experts = gate_ref.shape[1]
    for e in range(experts):
        raw = q_ref[:, e * HD:(e + 1) * HD]
        turned = raw * cosine + pltpu.roll(raw, HD // 2, 1) * sine_part
        queries = (turned * scale_factor).astype(jnp.bfloat16)
        scores = jnp.dot(queries, keys, preferred_element_type=jnp.float32)
        scores = jnp.where(allowed, scores, -1e30)
        top = jnp.max(scores, axis=1, keepdims=True)
        raised = jnp.exp(scores - top)
        inverse = 1.0 / jnp.sum(raised, axis=1, keepdims=True)
        probabilities = (raised * inverse).astype(jnp.bfloat16)
        attended = jnp.dot(probabilities, values, preferred_element_type=jnp.float32)
        out_ref[:, e * HD:(e + 1) * HD] = (attended * gate_ref[:, e:e + 1]).astype(out_ref.dtype)


def rope_tables(positions):
    half_width = HD // 2
    frequency = 10000.0 ** (-jnp.arange(half_width, dtype=jnp.float32) / half_width)
    angles = positions.astype(jnp.float32)[:, None] * frequency[None, :]
    cosine = jnp.cos(angles)
    sine_part = jnp.sin(angles)
    return (
        jnp.concatenate([cosine, cosine], axis=1),
        jnp.concatenate([-sine_part, sine_part], axis=1),
    )


def attend_window(raw_queries, positions, keys, values, segment_ids, gate_here):
    tokens, width = raw_queries.shape
    experts = width // HD
    blocks = tokens // CHUNK
    window = min(blocks, SEG_MOST // CHUNK + 1)
    cosine, sine_part = rope_tables(positions)
    seg_cols = segment_ids.reshape(tokens, 1)
    seg_row = segment_ids.reshape(1, tokens)
    return pl.pallas_call(
        lambda *refs: attention_kernel(window, *refs),
        grid=(blocks,),
        in_specs=[
            pl.BlockSpec((CHUNK, width), lambda i: (i, 0)),
            pl.BlockSpec((CHUNK, HD), lambda i: (i, 0)),
            pl.BlockSpec((CHUNK, HD), lambda i: (i, 0)),
            pl.BlockSpec((HD, tokens), lambda i: (0, 0)),
            pl.BlockSpec((tokens, HD), lambda i: (0, 0)),
            pl.BlockSpec((CHUNK, 1), lambda i: (i, 0)),
            pl.BlockSpec((1, tokens), lambda i: (0, 0)),
            pl.BlockSpec((CHUNK, experts), lambda i: (i, 0)),
        ],
        out_specs=pl.BlockSpec((CHUNK, width), lambda i: (i, 0)),
        out_shape=jax.ShapeDtypeStruct((tokens, width), jnp.bfloat16),
        cost_estimate=pl.CostEstimate(
            flops=4 * tokens * window * CHUNK * width,
            transcendentals=tokens * window * CHUNK * experts,
            bytes_accessed=tokens * width * 6 + 2 * tokens * HD * 2 + 2 * tokens * HD * 4,
        ),
    )(raw_queries, cosine, sine_part, jnp.transpose(keys), values, seg_cols, seg_row, gate_here)


def gather_from_all(block, axis):
    size = lax.axis_size(axis)
    bits = size.bit_length() - 1
    assert 1 << bits == size
    me = lax.axis_index(axis)
    rows, width = block.shape
    parts = REDUCE_PARTS if width % REDUCE_PARTS == 0 else 1
    piece = width // parts
    outs = []
    for j, forward in enumerate(bit_orders(bits, parts)):
        order = forward[::-1]
        current = block[:, j * piece:(j + 1) * piece]
        for k in order:
            got = lax.ppermute(current, axis, [(i, i ^ (1 << k)) for i in range(size)])
            upper = ((me >> k) & 1) == 1
            current = jnp.concatenate(
                [jnp.where(upper, got, current), jnp.where(upper, current, got)], axis=0
            )
        cube = current.reshape((2,) * bits + (rows, piece))
        old_axis = {order[bits - 1 - a]: a for a in range(bits)}
        cube = jnp.transpose(cube, [old_axis[bits - 1 - a] for a in range(bits)] + [bits, bits + 1])
        outs.append(cube.reshape(size * rows, piece))
    return jnp.concatenate(outs, axis=1)


def local(
    hidden,
    norm_gain,
    router_weight,
    kv_weight,
    query_weight,
    out_weight,
    routes,
    segment_ids,
    page_table,
    kv_cache,
):
    device_index = lax.axis_index("tensor")
    token_count = routes.shape[0]
    normed = gather_from_all(normalize(hidden, norm_gain), "tensor")
    gates = gate_table(normed, router_weight, routes)
    positions = positions_of(segment_ids)
    kv_width = kv_weight.shape[1]
    block_count = kv_width // HD
    own_rows = project_kv(normed, kv_weight, positions, device_index * block_count)
    new_cache = write_pages(kv_cache, page_table, own_rows.reshape(page_table.shape[0], PAGE, kv_width))
    partner_rows = swapped(own_rows, "tensor", 0)
    leading_first = device_index % 2 == 0
    key_rows = jnp.where(leading_first, own_rows, partner_rows)
    value_rows = jnp.where(leading_first, partner_rows, own_rows)
    pair_count = query_weight.shape[1] // HD
    raw_queries = jnp.dot(normed, query_weight, preferred_element_type=jnp.float32)
    first_expert = (device_index * pair_count) % EA
    gate_here = gates[:, :pair_count]
    for group in range(1, EA // pair_count):
        gate_here = jnp.where(
            first_expert == group * pair_count,
            gates[:, group * pair_count:(group + 1) * pair_count],
            gate_here,
        )
    flat = attend_window(raw_queries, positions, key_rows, value_rows, segment_ids, gate_here)
    partial = jnp.dot(flat, out_weight, preferred_element_type=jnp.float32).astype(jnp.bfloat16)
    reduced = reduce_to_owner(partial, "tensor").astype(jnp.float32)
    attended_out = (hidden.astype(jnp.float32) + reduced).astype(jnp.bfloat16)
    return (attended_out, new_cache)


def solution(mesh):
    placed = (
        P(("dp", "tensor"), None),
        P(),
        P(),
        P(None, "tensor"),
        P(None, "tensor"),
        P("tensor", None),
        P("dp", None),
        P("dp"),
        P("dp"),
        P("dp", None, "tensor"),
    )
    return jax.shard_map(
        local,
        mesh=mesh,
        in_specs=placed,
        out_specs=(P(("dp", "tensor"), None), P("dp", None, "tensor")),
        check_vma=False,
    )
```

```python
import jax
import jax.numpy as jnp
from jax import lax
from jax.experimental import pallas as pl
from jax.experimental.pallas import tpu as pltpu
from jax.sharding import PartitionSpec as P

D = 2048
HD = 128
EA = 8
PAGE = 128
REDUCE_PARTS = 4
SEG_MOST = 512
CHUNK = 256


def swapped(array, axis, bit):
    return lax.ppermute(array, axis, [(i, i ^ 1 << bit) for i in range(lax.axis_size(axis))])


def normalize(hidden, norm_gain):
    values = hidden.astype(jnp.float32)
    factor = lax.rsqrt(jnp.mean(values * values, axis=-1, keepdims=True) + 1e-05)
    return (values * factor * norm_gain.astype(jnp.float32)).astype(jnp.bfloat16)


def gate_table(normed, router_weight, routes):
    logits = jnp.dot(normed, router_weight, preferred_element_type=jnp.float32)
    expert_ids = jnp.arange(router_weight.shape[1], dtype=jnp.int32)
    onehot = routes[:, :, None] == expert_ids[None, None, :]
    chosen = jnp.sum(jnp.where(onehot, logits[:, None, :], 0.0), axis=2)
    weights = jax.nn.softmax(chosen, axis=-1)
    return jnp.sum(jnp.where(onehot, weights[:, :, None], 0.0), axis=1)


def positions_of(segment_ids):
    index_row = jnp.arange(segment_ids.shape[0], dtype=jnp.int32)
    starts_here = jnp.concatenate([jnp.ones((1,), dtype=bool), segment_ids[1:] != segment_ids[:-1]])
    segment_start = lax.cummax(jnp.where(starts_here, index_row, 0), axis=0)
    return index_row - segment_start


def rotate(values, positions):
    half_width = values.shape[-1] // 2
    frequency = 10000.0 ** (-jnp.arange(half_width, dtype=jnp.float32) / half_width)
    angles = positions.astype(jnp.float32)[:, None] * frequency[None, :]
    angles = angles.reshape((values.shape[0],) + (1,) * (values.ndim - 2) + (half_width,))
    cosine = jnp.cos(angles)
    sine_part = jnp.sin(angles)
    leading = values[..., :half_width]
    trailing = values[..., half_width:]
    return jnp.concatenate(
        [leading * cosine - trailing * sine_part, trailing * cosine + leading * sine_part], axis=-1
    )


def project_kv(normed, weight, positions, first_block):
    projected = jnp.dot(normed, weight, preferred_element_type=jnp.float32)
    block_total = weight.shape[1] // HD
    blocks = projected.reshape(normed.shape[0], block_total, HD)
    block_index = first_block + jnp.arange(block_total, dtype=jnp.int32)
    turned = rotate(blocks, positions)
    chosen = jnp.where((block_index % 2 == 0)[None, :, None], turned, blocks)
    return chosen.astype(jnp.bfloat16).reshape(normed.shape[0], weight.shape[1])


def write_pages(kv_cache, page_table, rows):
    pages = jnp.arange(kv_cache.shape[0], dtype=jnp.int32)
    hit = page_table[None, :] == pages[:, None]
    placed = jnp.einsum(
        "pb,brc->prc", hit.astype(rows.dtype), rows, preferred_element_type=jnp.float32
    ).astype(kv_cache.dtype)
    return jnp.where(jnp.any(hit, axis=1)[:, None, None], placed, kv_cache)


def bit_orders(bits, parts):
    rest = list(range(1, bits))
    if not rest:
        return [[0]] * parts
    return [[0] + rest[j % len(rest):] + rest[:j % len(rest)] for j in range(parts)]


def reduce_to_owner(partial, axis):
    size = lax.axis_size(axis)
    bits = size.bit_length() - 1
    assert 1 << bits == size
    me = lax.axis_index(axis)
    rows, width = partial.shape
    block = rows // size
    parts = REDUCE_PARTS if width % REDUCE_PARTS == 0 else 1
    piece = width // parts
    outs = []
    for j, order in enumerate(bit_orders(bits, parts)):
        cols = partial[:, j * piece:(j + 1) * piece]
        cube = cols.reshape((2,) * bits + (block, piece))
        cube = jnp.transpose(cube, [bits - 1 - k for k in order] + [bits, bits + 1])
        current = cube.reshape(rows, piece)
        for k in order:
            half = current.shape[0] // 2
            mine = (me >> k) & 1
            keep = lax.dynamic_slice_in_dim(current, mine * half, half, 0)
            send = lax.dynamic_slice_in_dim(current, (1 - mine) * half, half, 0)
            got = lax.ppermute(send, axis, [(i, i ^ (1 << k)) for i in range(size)])
            current = (keep.astype(jnp.float32) + got.astype(jnp.float32)).astype(jnp.bfloat16)
        outs.append(current)
    return jnp.concatenate(outs, axis=1)


def attention_kernel(window, q_ref, cos_ref, sin_ref, k_ref, v_ref, qseg_ref, kseg_ref, gate_ref, out_ref):
    chunk = pl.program_id(0)
    blocks = pl.num_programs(0)
    start_block = jnp.clip(chunk - (window - 1), 0, blocks - window)
    start = pl.multiple_of(start_block * CHUNK, CHUNK)
    span = window * CHUNK
    keys = k_ref[pl.ds(start, span), :]
    values = v_ref[pl.ds(start, span), :]
    key_seg = kseg_ref[:, pl.ds(start, span)]
    query_seg = qseg_ref[...]
    query_index = chunk * CHUNK + lax.broadcasted_iota(jnp.int32, (CHUNK, span), 0)
    key_index = start + lax.broadcasted_iota(jnp.int32, (CHUNK, span), 1)
    allowed = (query_seg == key_seg) & (key_index <= query_index)
    cosine = cos_ref[...]
    sine_part = sin_ref[...]
    scale_factor = HD ** (-0.5)
    experts = gate_ref.shape[1]
    for e in range(experts):
        raw = q_ref[:, e * HD:(e + 1) * HD]
        turned = raw * cosine + pltpu.roll(raw, HD // 2, 1) * sine_part
        queries = (turned * scale_factor).astype(jnp.bfloat16)
        scores = lax.dot_general(
            queries, keys, (((1,), (1,)), ((), ())), preferred_element_type=jnp.float32
        )
        scores = jnp.where(allowed, scores, -1e30)
        top = jnp.max(scores, axis=1, keepdims=True)
        raised = jnp.exp(scores - top)
        inverse = 1.0 / jnp.sum(raised, axis=1, keepdims=True)
        probabilities = (raised * inverse).astype(jnp.bfloat16)
        attended = jnp.dot(probabilities, values, preferred_element_type=jnp.float32)
        out_ref[:, e * HD:(e + 1) * HD] = (attended * gate_ref[:, e:e + 1]).astype(out_ref.dtype)


def rope_tables(positions):
    half_width = HD // 2
    frequency = 10000.0 ** (-jnp.arange(half_width, dtype=jnp.float32) / half_width)
    angles = positions.astype(jnp.float32)[:, None] * frequency[None, :]
    cosine = jnp.cos(angles)
    sine_part = jnp.sin(angles)
    return (
        jnp.concatenate([cosine, cosine], axis=1),
        jnp.concatenate([-sine_part, sine_part], axis=1),
    )


def attend_window(raw_queries, positions, keys, values, segment_ids, gate_here):
    tokens, width = raw_queries.shape
    experts = width // HD
    blocks = tokens // CHUNK
    window = min(blocks, SEG_MOST // CHUNK + 1)
    cosine, sine_part = rope_tables(positions)
    seg_cols = segment_ids.reshape(tokens, 1)
    seg_row = segment_ids.reshape(1, tokens)
    return pl.pallas_call(
        lambda *refs: attention_kernel(window, *refs),
        grid=(blocks,),
        in_specs=[
            pl.BlockSpec((CHUNK, width), lambda i: (i, 0)),
            pl.BlockSpec((CHUNK, HD), lambda i: (i, 0)),
            pl.BlockSpec((CHUNK, HD), lambda i: (i, 0)),
            pl.BlockSpec((tokens, HD), lambda i: (0, 0)),
            pl.BlockSpec((tokens, HD), lambda i: (0, 0)),
            pl.BlockSpec((CHUNK, 1), lambda i: (i, 0)),
            pl.BlockSpec((1, tokens), lambda i: (0, 0)),
            pl.BlockSpec((CHUNK, experts), lambda i: (i, 0)),
        ],
        out_specs=pl.BlockSpec((CHUNK, width), lambda i: (i, 0)),
        out_shape=jax.ShapeDtypeStruct((tokens, width), jnp.bfloat16),
        cost_estimate=pl.CostEstimate(
            flops=4 * tokens * window * CHUNK * width,
            transcendentals=tokens * window * CHUNK * experts,
            bytes_accessed=tokens * width * 6 + 2 * tokens * HD * 2 + 2 * tokens * HD * 4,
        ),
    )(raw_queries, cosine, sine_part, keys, values, seg_cols, seg_row, gate_here)


def gather_from_all(block, axis):
    size = lax.axis_size(axis)
    bits = size.bit_length() - 1
    assert 1 << bits == size
    me = lax.axis_index(axis)
    rows, width = block.shape
    parts = REDUCE_PARTS if width % REDUCE_PARTS == 0 else 1
    piece = width // parts
    outs = []
    for j, forward in enumerate(bit_orders(bits, parts)):
        order = forward[::-1]
        current = block[:, j * piece:(j + 1) * piece]
        for k in order:
            got = lax.ppermute(current, axis, [(i, i ^ (1 << k)) for i in range(size)])
            upper = ((me >> k) & 1) == 1
            current = jnp.concatenate(
                [jnp.where(upper, got, current), jnp.where(upper, current, got)], axis=0
            )
        cube = current.reshape((2,) * bits + (rows, piece))
        old_axis = {order[bits - 1 - a]: a for a in range(bits)}
        cube = jnp.transpose(cube, [old_axis[bits - 1 - a] for a in range(bits)] + [bits, bits + 1])
        outs.append(cube.reshape(size * rows, piece))
    return jnp.concatenate(outs, axis=1)


def local(
    hidden,
    norm_gain,
    router_weight,
    kv_weight,
    query_weight,
    out_weight,
    routes,
    segment_ids,
    page_table,
    kv_cache,
):
    device_index = lax.axis_index("tensor")
    token_count = routes.shape[0]
    normed = gather_from_all(normalize(hidden, norm_gain), "tensor")
    gates = gate_table(normed, router_weight, routes)
    positions = positions_of(segment_ids)
    kv_width = kv_weight.shape[1]
    block_count = kv_width // HD
    own_rows = project_kv(normed, kv_weight, positions, device_index * block_count)
    new_cache = write_pages(kv_cache, page_table, own_rows.reshape(page_table.shape[0], PAGE, kv_width))
    partner_rows = swapped(own_rows, "tensor", 0)
    leading_first = device_index % 2 == 0
    key_rows = jnp.where(leading_first, own_rows, partner_rows)
    value_rows = jnp.where(leading_first, partner_rows, own_rows)
    pair_count = query_weight.shape[1] // HD
    raw_queries = jnp.dot(normed, query_weight, preferred_element_type=jnp.float32)
    first_expert = (device_index * pair_count) % EA
    gate_here = gates[:, :pair_count]
    for group in range(1, EA // pair_count):
        gate_here = jnp.where(
            first_expert == group * pair_count,
            gates[:, group * pair_count:(group + 1) * pair_count],
            gate_here,
        )
    flat = attend_window(raw_queries, positions, key_rows, value_rows, segment_ids, gate_here)
    partial = jnp.dot(flat, out_weight, preferred_element_type=jnp.float32).astype(jnp.bfloat16)
    reduced = reduce_to_owner(partial, "tensor").astype(jnp.float32)
    attended_out = (hidden.astype(jnp.float32) + reduced).astype(jnp.bfloat16)
    return (attended_out, new_cache)


def solution(mesh):
    placed = (
        P(("dp", "tensor"), None),
        P(),
        P(),
        P(None, "tensor"),
        P(None, "tensor"),
        P("tensor", None),
        P("dp", None),
        P("dp"),
        P("dp"),
        P("dp", None, "tensor"),
    )
    return jax.shard_map(
        local,
        mesh=mesh,
        in_specs=placed,
        out_specs=(P(("dp", "tensor"), None), P("dp", None, "tensor")),
        check_vma=False,
    )
```

```python
import jax
import jax.numpy as jnp
from jax import lax
from jax.experimental import pallas as pl
from jax.experimental.pallas import tpu as pltpu
from jax.sharding import PartitionSpec as P

D = 2048
HD = 128
EA = 8
PAGE = 128
REDUCE_PARTS = 4
SEG_MOST = 512
CHUNK = 256


def swapped(array, axis, bit):
    return lax.ppermute(array, axis, [(i, i ^ 1 << bit) for i in range(lax.axis_size(axis))])


def normalize(hidden, norm_gain):
    values = hidden.astype(jnp.float32)
    factor = lax.rsqrt(jnp.mean(values * values, axis=-1, keepdims=True) + 1e-05)
    return (values * factor * norm_gain.astype(jnp.float32)).astype(jnp.bfloat16)


def gate_table(normed, router_weight, routes):
    logits = jnp.dot(normed, router_weight, preferred_element_type=jnp.float32)
    expert_ids = jnp.arange(router_weight.shape[1], dtype=jnp.int32)
    onehot = routes[:, :, None] == expert_ids[None, None, :]
    chosen = jnp.sum(jnp.where(onehot, logits[:, None, :], 0.0), axis=2)
    weights = jax.nn.softmax(chosen, axis=-1)
    return jnp.sum(jnp.where(onehot, weights[:, :, None], 0.0), axis=1)


def positions_of(segment_ids):
    index_row = jnp.arange(segment_ids.shape[0], dtype=jnp.int32)
    starts_here = jnp.concatenate([jnp.ones((1,), dtype=bool), segment_ids[1:] != segment_ids[:-1]])
    segment_start = lax.cummax(jnp.where(starts_here, index_row, 0), axis=0)
    return index_row - segment_start


def rotate(values, positions):
    half_width = values.shape[-1] // 2
    frequency = 10000.0 ** (-jnp.arange(half_width, dtype=jnp.float32) / half_width)
    angles = positions.astype(jnp.float32)[:, None] * frequency[None, :]
    angles = angles.reshape((values.shape[0],) + (1,) * (values.ndim - 2) + (half_width,))
    cosine = jnp.cos(angles)
    sine_part = jnp.sin(angles)
    leading = values[..., :half_width]
    trailing = values[..., half_width:]
    return jnp.concatenate(
        [leading * cosine - trailing * sine_part, trailing * cosine + leading * sine_part], axis=-1
    )


def project_kv(normed, weight, positions, first_block):
    projected = jnp.dot(normed, weight, preferred_element_type=jnp.float32)
    block_total = weight.shape[1] // HD
    blocks = projected.reshape(normed.shape[0], block_total, HD)
    block_index = first_block + jnp.arange(block_total, dtype=jnp.int32)
    turned = rotate(blocks, positions)
    chosen = jnp.where((block_index % 2 == 0)[None, :, None], turned, blocks)
    return chosen.astype(jnp.bfloat16).reshape(normed.shape[0], weight.shape[1])


def write_pages(kv_cache, page_table, rows):
    for block in range(rows.shape[0]):
        kv_cache = lax.dynamic_update_slice_in_dim(kv_cache, rows[block:block + 1], page_table[block], 0)
    return kv_cache


def bit_orders(bits, parts):
    rest = list(range(1, bits))
    if not rest:
        return [[0]] * parts
    return [[0] + rest[j % len(rest):] + rest[:j % len(rest)] for j in range(parts)]


def reduce_to_owner(partial, axis):
    size = lax.axis_size(axis)
    bits = size.bit_length() - 1
    assert 1 << bits == size
    me = lax.axis_index(axis)
    rows, width = partial.shape
    block = rows // size
    parts = REDUCE_PARTS if width % REDUCE_PARTS == 0 else 1
    piece = width // parts
    outs = []
    for j, order in enumerate(bit_orders(bits, parts)):
        cols = partial[:, j * piece:(j + 1) * piece]
        cube = cols.reshape((2,) * bits + (block, piece))
        cube = jnp.transpose(cube, [bits - 1 - k for k in order] + [bits, bits + 1])
        current = cube.reshape(rows, piece)
        for k in order:
            half = current.shape[0] // 2
            mine = (me >> k) & 1
            keep = lax.dynamic_slice_in_dim(current, mine * half, half, 0)
            send = lax.dynamic_slice_in_dim(current, (1 - mine) * half, half, 0)
            got = lax.ppermute(send, axis, [(i, i ^ (1 << k)) for i in range(size)])
            current = (keep.astype(jnp.float32) + got.astype(jnp.float32)).astype(jnp.bfloat16)
        outs.append(current)
    return jnp.concatenate(outs, axis=1)


def attention_kernel(window, q_ref, cos_ref, sin_ref, k_ref, v_ref, qseg_ref, kseg_ref, gate_ref, out_ref):
    chunk = pl.program_id(0)
    blocks = pl.num_programs(0)
    start_block = jnp.clip(chunk - (window - 1), 0, blocks - window)
    start = pl.multiple_of(start_block * CHUNK, CHUNK)
    span = window * CHUNK
    keys = k_ref[pl.ds(start, span), :]
    values = v_ref[pl.ds(start, span), :]
    key_seg = kseg_ref[:, pl.ds(start, span)]
    query_seg = qseg_ref[...]
    query_index = chunk * CHUNK + lax.broadcasted_iota(jnp.int32, (CHUNK, span), 0)
    key_index = start + lax.broadcasted_iota(jnp.int32, (CHUNK, span), 1)
    allowed = (query_seg == key_seg) & (key_index <= query_index)
    cosine = cos_ref[...]
    sine_part = sin_ref[...]
    scale_factor = HD ** (-0.5)
    experts = gate_ref.shape[1]
    for e in range(experts):
        raw = q_ref[:, e * HD:(e + 1) * HD]
        turned = raw * cosine + pltpu.roll(raw, HD // 2, 1) * sine_part
        queries = (turned * scale_factor).astype(jnp.bfloat16)
        scores = lax.dot_general(
            queries, keys, (((1,), (1,)), ((), ())), preferred_element_type=jnp.float32
        )
        scores = jnp.where(allowed, scores, -1e30)
        top = jnp.max(scores, axis=1, keepdims=True)
        raised = jnp.exp(scores - top)
        inverse = 1.0 / jnp.sum(raised, axis=1, keepdims=True)
        probabilities = (raised * inverse).astype(jnp.bfloat16)
        attended = jnp.dot(probabilities, values, preferred_element_type=jnp.float32)
        out_ref[:, e * HD:(e + 1) * HD] = (attended * gate_ref[:, e:e + 1]).astype(out_ref.dtype)


def rope_tables(positions):
    half_width = HD // 2
    frequency = 10000.0 ** (-jnp.arange(half_width, dtype=jnp.float32) / half_width)
    angles = positions.astype(jnp.float32)[:, None] * frequency[None, :]
    cosine = jnp.cos(angles)
    sine_part = jnp.sin(angles)
    return (
        jnp.concatenate([cosine, cosine], axis=1),
        jnp.concatenate([-sine_part, sine_part], axis=1),
    )


def attend_window(raw_queries, positions, keys, values, segment_ids, gate_here):
    tokens, width = raw_queries.shape
    experts = width // HD
    blocks = tokens // CHUNK
    window = min(blocks, SEG_MOST // CHUNK + 1)
    cosine, sine_part = rope_tables(positions)
    seg_cols = segment_ids.reshape(tokens, 1)
    seg_row = segment_ids.reshape(1, tokens)
    return pl.pallas_call(
        lambda *refs: attention_kernel(window, *refs),
        grid=(blocks,),
        in_specs=[
            pl.BlockSpec((CHUNK, width), lambda i: (i, 0)),
            pl.BlockSpec((CHUNK, HD), lambda i: (i, 0)),
            pl.BlockSpec((CHUNK, HD), lambda i: (i, 0)),
            pl.BlockSpec((tokens, HD), lambda i: (0, 0)),
            pl.BlockSpec((tokens, HD), lambda i: (0, 0)),
            pl.BlockSpec((CHUNK, 1), lambda i: (i, 0)),
            pl.BlockSpec((1, tokens), lambda i: (0, 0)),
            pl.BlockSpec((CHUNK, experts), lambda i: (i, 0)),
        ],
        out_specs=pl.BlockSpec((CHUNK, width), lambda i: (i, 0)),
        out_shape=jax.ShapeDtypeStruct((tokens, width), jnp.bfloat16),
        cost_estimate=pl.CostEstimate(
            flops=4 * tokens * window * CHUNK * width,
            transcendentals=tokens * window * CHUNK * experts,
            bytes_accessed=tokens * width * 6 + 2 * tokens * HD * 2 + 2 * tokens * HD * 4,
        ),
    )(raw_queries, cosine, sine_part, keys, values, seg_cols, seg_row, gate_here)


def gather_from_all(block, axis):
    size = lax.axis_size(axis)
    bits = size.bit_length() - 1
    assert 1 << bits == size
    me = lax.axis_index(axis)
    rows, width = block.shape
    parts = REDUCE_PARTS if width % REDUCE_PARTS == 0 else 1
    piece = width // parts
    outs = []
    for j, forward in enumerate(bit_orders(bits, parts)):
        order = forward[::-1]
        current = block[:, j * piece:(j + 1) * piece]
        for k in order:
            got = lax.ppermute(current, axis, [(i, i ^ (1 << k)) for i in range(size)])
            upper = ((me >> k) & 1) == 1
            current = jnp.concatenate(
                [jnp.where(upper, got, current), jnp.where(upper, current, got)], axis=0
            )
        cube = current.reshape((2,) * bits + (rows, piece))
        old_axis = {order[bits - 1 - a]: a for a in range(bits)}
        cube = jnp.transpose(cube, [old_axis[bits - 1 - a] for a in range(bits)] + [bits, bits + 1])
        outs.append(cube.reshape(size * rows, piece))
    return jnp.concatenate(outs, axis=1)


def local(
    hidden,
    norm_gain,
    router_weight,
    kv_weight,
    query_weight,
    out_weight,
    routes,
    segment_ids,
    page_table,
    kv_cache,
):
    device_index = lax.axis_index("tensor")
    token_count = routes.shape[0]
    normed = gather_from_all(normalize(hidden, norm_gain), "tensor")
    gates = gate_table(normed, router_weight, routes)
    positions = positions_of(segment_ids)
    kv_width = kv_weight.shape[1]
    block_count = kv_width // HD
    own_rows = project_kv(normed, kv_weight, positions, device_index * block_count)
    new_cache = write_pages(kv_cache, page_table, own_rows.reshape(page_table.shape[0], PAGE, kv_width))
    partner_rows = swapped(own_rows, "tensor", 0)
    leading_first = device_index % 2 == 0
    key_rows = jnp.where(leading_first, own_rows, partner_rows)
    value_rows = jnp.where(leading_first, partner_rows, own_rows)
    pair_count = query_weight.shape[1] // HD
    raw_queries = jnp.dot(normed, query_weight, preferred_element_type=jnp.float32)
    first_expert = (device_index * pair_count) % EA
    gate_here = gates[:, :pair_count]
    for group in range(1, EA // pair_count):
        gate_here = jnp.where(
            first_expert == group * pair_count,
            gates[:, group * pair_count:(group + 1) * pair_count],
            gate_here,
        )
    flat = attend_window(raw_queries, positions, key_rows, value_rows, segment_ids, gate_here)
    partial = jnp.dot(flat, out_weight, preferred_element_type=jnp.float32).astype(jnp.bfloat16)
    reduced = reduce_to_owner(partial, "tensor").astype(jnp.float32)
    attended_out = (hidden.astype(jnp.float32) + reduced).astype(jnp.bfloat16)
    return (attended_out, new_cache)


def solution(mesh):
    placed = (
        P(("dp", "tensor"), None),
        P(),
        P(),
        P(None, "tensor"),
        P(None, "tensor"),
        P("tensor", None),
        P("dp", None),
        P("dp"),
        P("dp"),
        P("dp", None, "tensor"),
    )
    return jax.shard_map(
        local,
        mesh=mesh,
        in_specs=placed,
        out_specs=(P(("dp", "tensor"), None), P("dp", None, "tensor")),
        check_vma=False,
    )
```
